512 devices in a mesh: clip: 4 (over y), st: 32 (over x_hi, z), fsdp: 4 (over x_lo, core).
Axes of the slice: x: 4 (x_hi: 2, x_lo: 2; x = x_hi * 2 + x_lo), y: 4, z: 16, core: 2. Of those that a mesh axis runs over, the one named last changes fastest.
Arguments:
- clip_tokens: bfloat16 [1024, 128, 1024], P(('clip', 'st'), 'fsdp'), parts along dimension 0, may hold values from -6 to 6
- w_spatial: bfloat16 [9, 1024, 512], P(None, ('st', 'fsdp')), may hold values from -0.0625 to 0.0625
- w_temporal: bfloat16 [3, 512, 1024], P(None, None, ('st', 'fsdp')), may hold values from -0.15625 to 0.15625
- frame_time: int32 [64], P('clip'), parts along dimension 0, may hold values from 0 to 15, each once
- dilation: int32 [32], P('clip'), parts along dimension 0, may hold values from 1 to 3
Outputs:
- block_out: bfloat16 [1024, 128, 1024], P(('clip', 'st'), 'fsdp'), parts along dimension 0
The draws below stay inside these ranges and needn't reach their ends.
There are 4 independent parts, one for each index of `clip`. The reference program is written for one: setup_inputs(seed, part) draws one part's arguments, and reference() takes and returns one part's arrays. A program takes and returns all parts, laid end to end along the dimension named above; an argument that names none is the same for every part. Nothing has to cross between parts.
Inputs may be any that keep to these rules, and one draw needn't show every extreme that they name: frame_time is a permutation of 0 to 15.
All inputs are finite; a program needn't handle non-finite values.
Results may differ from the reference program's by a relative error of at most 0.0049.
Values may be sent and summed in bfloat16 or wider, within the bound.
No kernel may reach another device: no remote copies, remote signals or barrier semaphores. Data moves between devices by JAX's collectives and lax.ppermute only.
A program may use at most 64 MiB of HBM per device.

```python
import jax
import jax.numpy as jnp
from jax import lax

WIDTH = 1024
INNER = 512
DGROUPS = 8
FRAMES = 16
ROWS = 16
COLS = 128


def touch_ends(entries, stream_key, low, top_value):
    dims = entries.shape
    index_at = [jax.random.randint(jax.random.fold_in(stream_key, axis), (), 0, dims[axis]) for axis in range(len(dims))]
    entries = entries.at[tuple(index_at)].set(low)
    longest = dims.index(max(dims))
    index_at[longest] = (index_at[longest] + 1) % dims[longest]
    return entries.at[tuple(index_at)].set(top_value)


def steps_of(key, dims, cuts, least, high):
    loudness = 1.0
    for position, blocks in cuts:
        draws = jax.random.uniform(jax.random.fold_in(jax.random.fold_in(key, 6), position), (blocks,), jnp.float32, least / len(cuts), high / len(cuts))
        loudness = loudness * jnp.repeat(jnp.exp(draws), dims[position] // blocks).reshape((-1,) + (1,) * (len(dims) - 1 - position))
    return loudness


def normal_values(own_key, dims, spread, most, cuts=(), kind=jnp.bfloat16):
    entries = jax.random.normal(own_key, dims, jnp.float32) * spread
    if len(cuts) > 0:
        entries = steps_of(own_key, dims, cuts, -0.22, 0.18) * entries
    return jnp.clip(entries, min=-most, max=most).astype(kind)


def setup_inputs(seed: int = 0, part: int = 0) -> dict:
    keys = jax.random.split(jax.random.key(seed), 6)
    part_keys = jax.random.split(jax.random.fold_in(keys[5], part), 6)
    clip_tokens = normal_values(part_keys[0], (FRAMES * ROWS, COLS, WIDTH), 1.0, 6.0, ((0, 32), (1, 4)))
    w_spatial = normal_values(keys[1], (9, WIDTH, INNER), (9 * WIDTH) ** -0.5, 0.0625, ((1, 128),))
    w_temporal = normal_values(keys[2], (3, INNER, WIDTH), (3 * INNER) ** -0.5, 0.15625, ((2, 128),))
    frame_time = jax.random.permutation(part_keys[3], FRAMES).astype(jnp.int32)
    dilation = touch_ends(jax.random.randint(part_keys[4], (DGROUPS,), 1, 4), jax.random.fold_in(part_keys[4], 1), 1, 3).astype(jnp.int32)
    return dict(clip_tokens=clip_tokens, w_spatial=w_spatial, w_temporal=w_temporal, frame_time=frame_time, dilation=dilation)


def reference(clip_tokens, w_spatial, w_temporal, frame_time, dilation):
    values = clip_tokens.astype(jnp.float32)
    average = lax.optimization_barrier(jnp.mean(values, axis=-1, keepdims=True))
    kernel_extent = lax.optimization_barrier(jnp.mean(jnp.square(values - average), axis=-1, keepdims=True))
    normed = ((values - average) * lax.rsqrt(kernel_extent + 1e-06)).astype(jnp.bfloat16)
    framed = normed.reshape(FRAMES, ROWS, COLS, WIDTH)
    padded = jnp.pad(framed, ((0, 0), (1, 1), (1, 1), (0, 0)))
    spatial = jnp.zeros((FRAMES * ROWS * COLS, INNER), jnp.float32)
    for row_tap in range(3):
        for column_kernel_tap in range(3):
            patches = padded[:, row_tap:row_tap + ROWS, column_kernel_tap:column_kernel_tap + COLS, :].reshape(-1, WIDTH)
            spatial = spatial + jnp.dot(patches, w_spatial[3 * row_tap + column_kernel_tap], preferred_element_type=jnp.float32)
    hidden = jax.nn.gelu(spatial).astype(jnp.bfloat16).reshape(FRAMES, ROWS * COLS, DGROUPS, INNER // DGROUPS)
    slot_of = jnp.zeros((FRAMES,), jnp.int32).at[frame_time].set(jnp.arange(FRAMES, dtype=jnp.int32))
    mixed = jnp.zeros((FRAMES * ROWS * COLS, WIDTH), jnp.float32)
    for tap_index in range(3):
        pieces = []
        for group_index in range(DGROUPS):
            target = frame_time + (tap_index - 1) * dilation[group_index]
            inside = ((target >= 0) & (target < FRAMES)).astype(hidden.dtype)
            source = slot_of[jnp.clip(target, 0, FRAMES - 1)].astype(jnp.int32)
            pieces.append(jnp.take(hidden[:, :, group_index, :], source, axis=0) * inside[:, None, None])
        shifted = jnp.stack(pieces, axis=2)
        mixed = mixed + jnp.dot(shifted.reshape(-1, INNER), w_temporal[tap_index], preferred_element_type=jnp.float32)
    rounded = lax.optimization_barrier(mixed.astype(jnp.bfloat16))
    summed = values + rounded.astype(jnp.float32).reshape(FRAMES * ROWS, COLS, WIDTH)
    return summed.astype(jnp.bfloat16)
```

```python
import jax
import jax.numpy as jnp
from jax import lax
from jax.sharding import PartitionSpec as P

DGROUPS = 8
FRAMES = 16
ROWS = 16
ST = ("xhi", "z")
FS = ("xlo", "core")


def padded_2(cells, sides, width):
    for axis, dim in sides:
        count = lax.axis_size(axis)
        ends = count - 1
        head = lax.slice_in_dim(cells, 0, width, axis=dim)
        tail = lax.slice_in_dim(cells, cells.shape[dim] - width, cells.shape[dim], axis=dim)
        cells = jnp.concatenate(
            [
                lax.ppermute(tail, axis, [(i, (i + 1) % count) for i in range(ends)]),
                cells,
                lax.ppermute(head, axis, [((i + 1) % count, i) for i in range(ends)]),
            ],
            axis=dim,
        )
    return cells


def partner(value, axis, distance):
    mask = 2**distance
    pairs = [(source, source ^ mask) for source in range(lax.axis_size(axis))]
    return lax.ppermute(value, axis, pairs)


def out_dot(panel, weight):
    return lax.dot_general(
        panel, weight, (((1,), (1,)), ((), ())), preferred_element_type=jnp.float32
    )


def gathered_weights(w_spatial, w_temporal):
    taps, block, middle = w_spatial.shape
    k_taps, _, out_block = w_temporal.shape
    cut = w_spatial.size
    flat = jnp.concatenate([w_spatial.reshape(-1), w_temporal.transpose(2, 0, 1).reshape(-1)])
    whole = lax.all_gather(flat, "z", axis=0)
    whole = lax.all_gather(whole, ("xhi", "xlo"), axis=0)
    whole = lax.all_gather(whole, "core", axis=0)
    n_core, n_x, n_z = whole.shape[:3]
    n_hi = lax.axis_size("xhi")
    lead = (n_core, n_hi, n_x // n_hi, n_z)
    spatial = whole[..., :cut].reshape(lead + (taps, block, middle))
    spatial = spatial.transpose(4, 1, 3, 2, 0, 5, 6).reshape(taps, -1, middle)
    temporal = whole[..., cut:].reshape(lead + (out_block, k_taps, middle))
    temporal = temporal.transpose(5, 1, 3, 2, 0, 4, 6).reshape(k_taps, -1, middle)
    return spatial, temporal


def shards(clip_tokens, w_spatial, w_temporal, frame_time, dilation):
    rows_dev, cols_dev, channels = clip_tokens.shape
    middle = w_spatial.shape[2]
    group_size = lax.axis_size(ST)
    values = clip_tokens.astype(jnp.float32)
    average = jnp.mean(values, axis=-1, keepdims=True)
    kernel_extent = jnp.mean(jnp.square(values - average), axis=-1, keepdims=True)
    normed = ((values - average) * lax.rsqrt(kernel_extent + 1e-06)).astype(jnp.bfloat16)
    widened = padded_2(normed, ((FS, 1),), 1)
    blank_row = jnp.zeros((1,) + widened.shape[1:], jnp.bfloat16)
    lower_half = lax.axis_index(ST) % 2 == 1
    outgoing = jnp.where(lower_half, widened[:1], widened[-1:])
    incoming = partner(outgoing, ST, 0)
    top_rim = jnp.where(lower_half, incoming, blank_row)
    bottom_rim = jnp.where(lower_half, blank_row, incoming)
    padded = jnp.concatenate([top_rim, widened, bottom_rim], axis=0)
    first_row = lax.axis_index(ST) * rows_dev
    in_frame = (first_row + jnp.arange(rows_dev, dtype=jnp.int32)) % ROWS
    windows = []
    for shift_amount in (-1, 0, 1):
        inside = ((in_frame + shift_amount >= 0) & (in_frame + shift_amount < ROWS)).astype(
            jnp.bfloat16
        )
        windows.append(
            padded[1 + shift_amount : 1 + shift_amount + rows_dev] * inside[:, None, None]
        )
    tokens = rows_dev * cols_dev
    initial = jnp.zeros((tokens, middle), jnp.float32)
    running = initial
    spatial_w, temporal_w = gathered_weights(w_spatial, w_temporal)
    portion = spatial_w
    span = portion.shape[1]
    for row_tap in range(3):
        for column_kernel_tap in range(3):
            patches = windows[row_tap][:, column_kernel_tap : column_kernel_tap + cols_dev, :]
            running = running + jnp.dot(
                patches.reshape(tokens, span),
                portion[3 * row_tap + column_kernel_tap],
                preferred_element_type=jnp.float32,
            )
    hidden = jax.nn.gelu(running).astype(jnp.bfloat16)
    pixel_values = ROWS * cols_dev
    block_length_span = min(tokens, pixel_values) // group_size
    depth_len = tokens // (group_size * block_length_span)
    arrived = lax.all_to_all(
        hidden.reshape(depth_len, group_size, block_length_span, middle),
        ST,
        split_axis=1,
        concat_axis=0,
        tiled=True,
    )
    per_pixel = pixel_values // group_size
    group_width = middle // DGROUPS
    frame_sequence = arrived.reshape(FRAMES, per_pixel, DGROUPS, group_width)
    offsets = (jnp.arange(3, dtype=jnp.int32) - 1)[None, :] * dilation[:, None]
    selector_matrix = (
        frame_time[None, None, None, :]
        == frame_time[None, None, :, None] + offsets[:, :, None, None]
    ).astype(jnp.bfloat16)
    stacked_panels = jnp.einsum(
        "gkfe,epgc->kfpgc", selector_matrix, frame_sequence, preferred_element_type=jnp.float32
    )
    stacked_panels = stacked_panels.astype(jnp.bfloat16).reshape(3, FRAMES * per_pixel, middle)
    portion = temporal_w
    result = out_dot(stacked_panels[0], portion[0])
    result = result + out_dot(stacked_panels[1], portion[1])
    mixed_out = (result + out_dot(stacked_panels[2], portion[2])).astype(jnp.bfloat16)
    returned = lax.all_to_all(
        mixed_out.reshape(group_size, depth_len, 1, block_length_span, channels),
        ST,
        split_axis=0,
        concat_axis=2,
        tiled=True,
    )
    update = returned.reshape(rows_dev, cols_dev, channels)
    return (values + update.astype(jnp.float32)).astype(jnp.bfloat16)


def solution(mesh):
    clips = mesh.shape["clip"]
    fine = jax.sharding.Mesh(
        mesh.devices.reshape(clips, 2, -1, 2, 2), ("clip", "xhi", "z", "xlo", "core")
    )
    return jax.shard_map(
        shards,
        mesh=fine,
        in_specs=(
            P(("clip", "xhi", "z"), ("xlo", "core"), None),
            P(None, ("xhi", "z", "xlo", "core"), None),
            P(None, None, ("xhi", "z", "xlo", "core")),
            P("clip"),
            P("clip"),
        ),
        out_specs=P(("clip", "xhi", "z"), ("xlo", "core"), None),
        check_vma=False,
    )
```

```python
import jax
import jax.numpy as jnp
from jax import lax
from jax.sharding import PartitionSpec as P

DGROUPS = 8
FRAMES = 16
ROWS = 16
ST = ("xhi", "zhi", "zlo")
FS = ("xlo", "core")
FRAME_AXES = ("xhi", "zhi")
ALL = ("xhi", "zhi", "zlo", "xlo", "core")


def padded_2(cells, sides, width):
    for axis, dim in sides:
        count = lax.axis_size(axis)
        ends = count - 1
        head = lax.slice_in_dim(cells, 0, width, axis=dim)
        tail = lax.slice_in_dim(cells, cells.shape[dim] - width, cells.shape[dim], axis=dim)
        cells = jnp.concatenate(
            [
                lax.ppermute(tail, axis, [(i, (i + 1) % count) for i in range(ends)]),
                cells,
                lax.ppermute(head, axis, [((i + 1) % count, i) for i in range(ends)]),
            ],
            axis=dim,
        )
    return cells


def partner(value, axis, distance):
    mask = 2**distance
    pairs = [(source, source ^ mask) for source in range(lax.axis_size(axis))]
    return lax.ppermute(value, axis, pairs)


def gathered_weights(w_spatial, w_temporal):
    flat = jnp.concatenate([w_spatial.reshape(-1), w_temporal.transpose(2, 0, 1).reshape(-1)])
    whole = lax.all_gather(flat, ("zhi", "zlo"), axis=0)
    whole = lax.all_gather(whole, ("xhi", "xlo"), axis=0)
    whole = lax.all_gather(whole, "core", axis=0)
    whole = whole.reshape(-1, flat.shape[0])
    cut = w_spatial.size
    spatial = whole[:, :cut].reshape(-1, w_spatial.shape[2])
    temporal = whole[:, cut:].reshape(-1, w_temporal.shape[0] * w_temporal.shape[1])
    return spatial, temporal


def channel_dims():
    return (
        lax.axis_size("xhi"),
        lax.axis_size("zhi") * lax.axis_size("zlo"),
        lax.axis_size("xlo"),
        lax.axis_size("core"),
    )


def to_gathered_order(cells, block):
    lead = cells.shape[:-1]
    n = len(lead)
    split = cells.reshape(lead + channel_dims() + (block,))
    order = tuple(range(n)) + (n + 3, n, n + 2, n + 1, n + 4)
    return split.transpose(order).reshape(lead + (-1, block))


def from_gathered_order(cells, block):
    lead = cells.shape[:-1]
    n = len(lead)
    xhi, z, xlo, core = channel_dims()
    split = cells.reshape(lead + (core, xhi, xlo, z, block))
    order = tuple(range(n)) + (n + 1, n + 3, n + 2, n, n + 4)
    return split.transpose(order).reshape(lead + (-1,))


def shards(clip_tokens, w_spatial, w_temporal, frame_time, dilation):
    rows_dev, cols_dev, channels = clip_tokens.shape
    middle = w_spatial.shape[2]
    block_in = w_spatial.shape[1]
    block_out = w_temporal.shape[2]
    spatial_w, temporal_w = gathered_weights(w_spatial, w_temporal)
    values = clip_tokens.astype(jnp.float32)
    average = jnp.mean(values, axis=-1, keepdims=True)
    kernel_extent = jnp.mean(jnp.square(values - average), axis=-1, keepdims=True)
    normed = ((values - average) * lax.rsqrt(kernel_extent + 1e-06)).astype(jnp.bfloat16)
    normed = to_gathered_order(normed, block_in).reshape(rows_dev, cols_dev, channels)
    widened = padded_2(normed, ((FS, 1),), 1)
    blank_row = jnp.zeros((1,) + widened.shape[1:], jnp.bfloat16)
    lower_half = lax.axis_index(ST) % 2 == 1
    outgoing = jnp.where(lower_half, widened[:1], widened[-1:])
    incoming = partner(outgoing, ST, 0)
    top_rim = jnp.where(lower_half, incoming, blank_row)
    bottom_rim = jnp.where(lower_half, blank_row, incoming)
    padded = jnp.concatenate([top_rim, widened, bottom_rim], axis=0)
    first_row = lax.axis_index(ST) * rows_dev
    in_frame = (first_row + jnp.arange(rows_dev, dtype=jnp.int32)) % ROWS
    windows = []
    for shift_amount in (-1, 0, 1):
        inside = ((in_frame + shift_amount >= 0) & (in_frame + shift_amount < ROWS)).astype(
            jnp.bfloat16
        )
        windows.append(
            padded[1 + shift_amount : 1 + shift_amount + rows_dev] * inside[:, None, None]
        )
    tokens = rows_dev * cols_dev
    taps = []
    for row_tap in range(3):
        for column_kernel_tap in range(3):
            patches = windows[row_tap][:, column_kernel_tap : column_kernel_tap + cols_dev, :]
            taps.append(patches.reshape(tokens, -1, block_in))
    im2col = jnp.stack(taps, axis=2).reshape(tokens, -1)
    running = jnp.dot(im2col, spatial_w, preferred_element_type=jnp.float32)
    hidden = jax.nn.gelu(running).astype(jnp.bfloat16)
    group_size = lax.axis_size(FRAME_AXES)
    per_pixel = tokens // group_size
    arrived = lax.all_to_all(
        hidden.reshape(group_size, per_pixel, middle), FRAME_AXES, 0, 0, tiled=True
    )
    group_width = middle // DGROUPS
    frame_sequence = arrived.reshape(FRAMES, per_pixel, DGROUPS, group_width)
    offsets = (jnp.arange(3, dtype=jnp.int32) - 1)[None, :] * dilation[:, None]
    selector_matrix = (
        frame_time[None, None, None, :]
        == frame_time[None, None, :, None] + offsets[:, :, None, None]
    ).astype(jnp.bfloat16)
    stacked_panels = jnp.einsum(
        "gkfe,epgc->fpkgc", selector_matrix, frame_sequence, preferred_element_type=jnp.float32
    )
    stacked_panels = stacked_panels.astype(jnp.bfloat16).reshape(FRAMES * per_pixel, -1)
    result = lax.dot_general(
        stacked_panels, temporal_w, (((1,), (1,)), ((), ())), preferred_element_type=jnp.float32
    )
    mixed_out = from_gathered_order(result.astype(jnp.bfloat16), block_out)
    returned = lax.all_to_all(
        mixed_out.reshape(group_size, per_pixel, channels), FRAME_AXES, 0, 0, tiled=True
    )
    update = returned.reshape(rows_dev, cols_dev, channels)
    return (values + update.astype(jnp.float32)).astype(jnp.bfloat16)


def solution(mesh):
    clips = mesh.shape["clip"]
    fine = jax.sharding.Mesh(
        mesh.devices.reshape(clips, 2, -1, 2, 2, 2), ("clip",) + ALL
    )
    return jax.shard_map(
        shards,
        mesh=fine,
        in_specs=(
            P(("clip",) + ST, FS, None),
            P(None, ALL, None),
            P(None, None, ALL),
            P("clip"),
            P("clip"),
        ),
        out_specs=P(("clip",) + ST, FS, None),
        check_vma=False,
    )
```

```python
import jax
import jax.numpy as jnp
from jax import lax
from jax.sharding import PartitionSpec as P

DGROUPS = 8
FRAMES = 16
ROWS = 16
ST = ("xhi", "zhi", "zlo")
FS = ("xlo", "core")
FRAME_AXES = ("xhi", "zhi")
ALL = ("xhi", "zhi", "zlo", "xlo", "core")


def padded_2(cells, sides, width):
    for axis, dim in sides:
        count = lax.axis_size(axis)
        ends = count - 1
        head = lax.slice_in_dim(cells, 0, width, axis=dim)
        tail = lax.slice_in_dim(cells, cells.shape[dim] - width, cells.shape[dim], axis=dim)
        cells = jnp.concatenate(
            [
                lax.ppermute(tail, axis, [(i, (i + 1) % count) for i in range(ends)]),
                cells,
                lax.ppermute(head, axis, [((i + 1) % count, i) for i in range(ends)]),
            ],
            axis=dim,
        )
    return cells


def partner(value, axis, distance):
    mask = 2**distance
    pairs = [(source, source ^ mask) for source in range(lax.axis_size(axis))]
    return lax.ppermute(value, axis, pairs)


def weight_rows(w_spatial, w_temporal):
    middle = w_spatial.shape[2]
    return jnp.concatenate(
        [w_spatial.reshape(-1, middle), w_temporal.transpose(2, 0, 1).reshape(-1, middle)], axis=0
    )


def channel_dims():
    return (
        lax.axis_size("xhi"),
        lax.axis_size("zhi") * lax.axis_size("zlo"),
        lax.axis_size("xlo"),
        lax.axis_size("core"),
    )


def to_gathered_order(cells, block):
    lead = cells.shape[:-1]
    n = len(lead)
    split = cells.reshape(lead + channel_dims() + (block,))
    order = tuple(range(n)) + (n + 3, n, n + 2, n + 1, n + 4)
    return split.transpose(order).reshape(lead + (-1, block))


def from_gathered_order(cells, block):
    lead = cells.shape[:-1]
    n = len(lead)
    xhi, z, xlo, core = channel_dims()
    split = cells.reshape(lead + (core, xhi, xlo, z, block))
    order = tuple(range(n)) + (n + 1, n + 3, n + 2, n, n + 4)
    return split.transpose(order).reshape(lead + (-1,))


def shards(clip_tokens, w_spatial, w_temporal, frame_time, dilation):
    rows_dev, cols_dev, channels = clip_tokens.shape
    middle = w_spatial.shape[2]
    block_in = w_spatial.shape[1]
    block_out = w_temporal.shape[2]
    spatial_rows = w_spatial.shape[0] * block_in
    along_z = lax.all_gather(weight_rows(w_spatial, w_temporal), ("zhi", "zlo"), axis=0)
    values = clip_tokens.astype(jnp.float32)
    average = jnp.mean(values, axis=-1, keepdims=True)
    kernel_extent = jnp.mean(jnp.square(values - average), axis=-1, keepdims=True)
    normed = ((values - average) * lax.rsqrt(kernel_extent + 1e-06)).astype(jnp.bfloat16)
    normed = to_gathered_order(normed, block_in).reshape(rows_dev, cols_dev, channels)
    widened = padded_2(normed, ((FS, 1),), 1)
    blank_row = jnp.zeros((1,) + widened.shape[1:], jnp.bfloat16)
    lower_half = lax.axis_index(ST) % 2 == 1
    outgoing = jnp.where(lower_half, widened[:1], widened[-1:])
    incoming = partner(outgoing, ST, 0)
    top_rim = jnp.where(lower_half, incoming, blank_row)
    bottom_rim = jnp.where(lower_half, blank_row, incoming)
    padded = jnp.concatenate([top_rim, widened, bottom_rim], axis=0)
    first_row = lax.axis_index(ST) * rows_dev
    in_frame = (first_row + jnp.arange(rows_dev, dtype=jnp.int32)) % ROWS
    windows = []
    for shift_amount in (-1, 0, 1):
        inside = ((in_frame + shift_amount >= 0) & (in_frame + shift_amount < ROWS)).astype(
            jnp.bfloat16
        )
        windows.append(
            padded[1 + shift_amount : 1 + shift_amount + rows_dev] * inside[:, None, None]
        )
    tokens = rows_dev * cols_dev
    taps = []
    for row_tap in range(3):
        for column_kernel_tap in range(3):
            patches = windows[row_tap][:, column_kernel_tap : column_kernel_tap + cols_dev, :]
            taps.append(patches.reshape(tokens, -1, block_in))
    im2col = jnp.stack(taps, axis=2).reshape(tokens, -1, spatial_rows)
    pad_rows = along_z.shape[1] - spatial_rows
    im2col = jnp.pad(im2col, ((0, 0), (0, 0), (0, pad_rows)))
    along_z, im2col = lax.optimization_barrier((along_z, im2col))
    whole = lax.all_gather(along_z, ("xhi", "xlo"), axis=0)
    whole = lax.all_gather(whole, "core", axis=0)
    whole = whole.reshape((-1,) + along_z.shape[1:])
    running = lax.dot_general(
        im2col, whole, (((1, 2), (0, 1)), ((), ())), preferred_element_type=jnp.float32
    )
    hidden = jax.nn.gelu(running).astype(jnp.bfloat16)
    group_size = lax.axis_size(FRAME_AXES)
    per_pixel = tokens // group_size
    arrived = lax.all_to_all(
        hidden.reshape(group_size, per_pixel, middle), FRAME_AXES, 0, 0, tiled=True
    )
    group_width = middle // DGROUPS
    frame_sequence = arrived.reshape(FRAMES, per_pixel, DGROUPS, group_width)
    offsets = (jnp.arange(3, dtype=jnp.int32) - 1)[None, :] * dilation[:, None]
    selector_matrix = (
        frame_time[None, None, None, :]
        == frame_time[None, None, :, None] + offsets[:, :, None, None]
    ).astype(jnp.bfloat16)
    stacked_panels = jnp.einsum(
        "gkfe,epgc->fpkgc", selector_matrix, frame_sequence, preferred_element_type=jnp.float32
    )
    stacked_panels = stacked_panels.astype(jnp.bfloat16).reshape(FRAMES * per_pixel, 3, middle)
    temporal_w = whole[:, spatial_rows:, :].reshape(whole.shape[0], block_out, 3, middle)
    result = lax.dot_general(
        stacked_panels, temporal_w, (((1, 2), (2, 3)), ((), ())), preferred_element_type=jnp.float32
    )
    result = result.reshape(FRAMES * per_pixel, channels)
    mixed_out = from_gathered_order(result.astype(jnp.bfloat16), block_out)
    returned = lax.all_to_all(
        mixed_out.reshape(group_size, per_pixel, channels), FRAME_AXES, 0, 0, tiled=True
    )
    update = returned.reshape(rows_dev, cols_dev, channels)
    return (values + update.astype(jnp.float32)).astype(jnp.bfloat16)


def solution(mesh):
    clips = mesh.shape["clip"]
    fine = jax.sharding.Mesh(
        mesh.devices.reshape(clips, 2, -1, 2, 2, 2), ("clip",) + ALL
    )
    return jax.shard_map(
        shards,
        mesh=fine,
        in_specs=(
            P(("clip",) + ST, FS, None),
            P(None, ALL, None),
            P(None, None, ALL),
            P("clip"),
            P("clip"),
        ),
        out_specs=P(("clip",) + ST, FS, None),
        check_vma=False,
    )
```

```python
import jax
import jax.numpy as jnp
from jax import lax
from jax.sharding import PartitionSpec as P

DGROUPS = 8
FRAMES = 16
ROWS = 16
ST = ("xhi", "zhi", "zlo")
FS = ("xlo", "core")
FRAME_AXES = ("xhi", "zhi")
ALL = ("xhi", "zhi", "zlo", "xlo", "core")


def padded_2(cells, sides, width):
    for axis, dim in sides:
        count = lax.axis_size(axis)
        ends = count - 1
        head = lax.slice_in_dim(cells, 0, width, axis=dim)
        tail = lax.slice_in_dim(cells, cells.shape[dim] - width, cells.shape[dim], axis=dim)
        cells = jnp.concatenate(
            [
                lax.ppermute(tail, axis, [(i, (i + 1) % count) for i in range(ends)]),
                cells,
                lax.ppermute(head, axis, [((i + 1) % count, i) for i in range(ends)]),
            ],
            axis=dim,
        )
    return cells


def partner(value, axis, distance):
    mask = 2**distance
    pairs = [(source, source ^ mask) for source in range(lax.axis_size(axis))]
    return lax.ppermute(value, axis, pairs)


def weight_rows(w_spatial, w_temporal):
    middle = w_spatial.shape[2]
    return jnp.concatenate(
        [w_spatial.reshape(-1, middle), w_temporal.transpose(2, 0, 1).reshape(-1, middle)], axis=0
    )


def channel_dims():
    return (
        lax.axis_size("xhi"),
        lax.axis_size("zhi") * lax.axis_size("zlo"),
        lax.axis_size("xlo"),
        lax.axis_size("core"),
    )


def to_gathered_order(cells, block):
    lead = cells.shape[:-1]
    n = len(lead)
    split = cells.reshape(lead + channel_dims() + (block,))
    order = tuple(range(n)) + (n + 3, n, n + 2, n + 1, n + 4)
    return split.transpose(order).reshape(lead + (-1, block))


def from_gathered_order(cells, block):
    lead = cells.shape[:-1]
    n = len(lead)
    xhi, z, xlo, core = channel_dims()
    split = cells.reshape(lead + (core, xhi, xlo, z, block))
    order = tuple(range(n)) + (n + 1, n + 3, n + 2, n, n + 4)
    return split.transpose(order).reshape(lead + (-1,))


def shards(clip_tokens, w_spatial, w_temporal, frame_time, dilation):
    rows_dev, cols_dev, channels = clip_tokens.shape
    middle = w_spatial.shape[2]
    block_in = w_spatial.shape[1]
    block_out = w_temporal.shape[2]
    spatial_rows = w_spatial.shape[0] * block_in
    along_z = lax.all_gather(weight_rows(w_spatial, w_temporal), ("zhi", "zlo"), axis=0)
    values = clip_tokens.astype(jnp.float32)
    average = jnp.mean(values, axis=-1, keepdims=True)
    kernel_extent = jnp.mean(jnp.square(values - average), axis=-1, keepdims=True)
    normed = ((values - average) * lax.rsqrt(kernel_extent + 1e-06)).astype(jnp.bfloat16)
    normed = to_gathered_order(normed, block_in).reshape(rows_dev, cols_dev, channels)
    widened = padded_2(normed, ((FS, 1),), 1)
    blank_row = jnp.zeros((1,) + widened.shape[1:], jnp.bfloat16)
    lower_half = lax.axis_index(ST) % 2 == 1
    outgoing = jnp.where(lower_half, widened[:1], widened[-1:])
    incoming = partner(outgoing, ST, 0)
    top_rim = jnp.where(lower_half, incoming, blank_row)
    bottom_rim = jnp.where(lower_half, blank_row, incoming)
    padded = jnp.concatenate([top_rim, widened, bottom_rim], axis=0)
    first_row = lax.axis_index(ST) * rows_dev
    in_frame = (first_row + jnp.arange(rows_dev, dtype=jnp.int32)) % ROWS
    windows = []
    for shift_amount in (-1, 0, 1):
        inside = ((in_frame + shift_amount >= 0) & (in_frame + shift_amount < ROWS)).astype(
            jnp.bfloat16
        )
        windows.append(
            padded[1 + shift_amount : 1 + shift_amount + rows_dev] * inside[:, None, None]
        )
    tokens = rows_dev * cols_dev
    along_z, *windows = lax.optimization_barrier((along_z, *windows))
    whole = lax.all_gather(along_z, ("xhi", "xlo"), axis=0)
    whole = lax.all_gather(whole, "core", axis=0)
    whole = whole.reshape((-1,) + along_z.shape[1:])
    running = jnp.zeros((tokens, middle), jnp.float32)
    for row_tap in range(3):
        for column_kernel_tap in range(3):
            tap = 3 * row_tap + column_kernel_tap
            patches = windows[row_tap][:, column_kernel_tap : column_kernel_tap + cols_dev, :]
            running = running + lax.dot_general(
                patches.reshape(tokens, -1, block_in),
                whole[:, tap * block_in : (tap + 1) * block_in, :],
                (((1, 2), (0, 1)), ((), ())),
                preferred_element_type=jnp.float32,
            )
    hidden = jax.nn.gelu(running).astype(jnp.bfloat16)
    group_size = lax.axis_size(FRAME_AXES)
    per_pixel = tokens // group_size
    arrived = lax.all_to_all(
        hidden.reshape(group_size, per_pixel, middle), FRAME_AXES, 0, 0, tiled=True
    )
    group_width = middle // DGROUPS
    frame_sequence = arrived.reshape(FRAMES, per_pixel, DGROUPS, group_width)
    offsets = (jnp.arange(3, dtype=jnp.int32) - 1)[None, :] * dilation[:, None]
    selector_matrix = (
        frame_time[None, None, None, :]
        == frame_time[None, None, :, None] + offsets[:, :, None, None]
    ).astype(jnp.bfloat16)
    stacked_panels = jnp.einsum(
        "gkfe,epgc->fpkgc", selector_matrix, frame_sequence, preferred_element_type=jnp.float32
    )
    stacked_panels = stacked_panels.astype(jnp.bfloat16).reshape(FRAMES * per_pixel, 3, middle)
    temporal_w = whole[:, spatial_rows:, :].reshape(whole.shape[0], block_out, 3, middle)
    result = lax.dot_general(
        stacked_panels, temporal_w, (((1, 2), (2, 3)), ((), ())), preferred_element_type=jnp.float32
    )
    result = result.reshape(FRAMES * per_pixel, channels)
    mixed_out = result.astype(jnp.bfloat16)
    returned = lax.all_to_all(
        mixed_out.reshape(group_size, per_pixel, channels), FRAME_AXES, 0, 0, tiled=True
    )
    update = from_gathered_order(returned.reshape(tokens, channels), block_out)
    update = update.reshape(rows_dev, cols_dev, channels)
    return (values + update.astype(jnp.float32)).astype(jnp.bfloat16)


def solution(mesh):
    clips = mesh.shape["clip"]
    fine = jax.sharding.Mesh(
        mesh.devices.reshape(clips, 2, -1, 2, 2, 2), ("clip",) + ALL
    )
    return jax.shard_map(
        shards,
        mesh=fine,
        in_specs=(
            P(("clip",) + ST, FS, None),
            P(None, ALL, None),
            P(None, None, ALL),
            P("clip"),
            P("clip"),
        ),
        out_specs=P(("clip",) + ST, FS, None),
        check_vma=False,
    )
```

```python
import jax
import jax.numpy as jnp
from jax import lax
from jax.sharding import PartitionSpec as P

DGROUPS = 8
FRAMES = 16
ROWS = 16
ST = ("xhi", "zhi", "zlo")
FS = ("xlo", "core")
FRAME_AXES = ("xhi", "zhi")
ALL = ("xhi", "zhi", "zlo", "xlo", "core")


def padded_2(cells, sides, width):
    for axis, dim in sides:
        count = lax.axis_size(axis)
        ends = count - 1
        head = lax.slice_in_dim(cells, 0, width, axis=dim)
        tail = lax.slice_in_dim(cells, cells.shape[dim] - width, cells.shape[dim], axis=dim)
        cells = jnp.concatenate(
            [
                lax.ppermute(tail, axis, [(i, (i + 1) % count) for i in range(ends)]),
                cells,
                lax.ppermute(head, axis, [((i + 1) % count, i) for i in range(ends)]),
            ],
            axis=dim,
        )
    return cells


def partner(value, axis, distance):
    mask = 2**distance
    pairs = [(source, source ^ mask) for source in range(lax.axis_size(axis))]
    return lax.ppermute(value, axis, pairs)


def weight_rows(w_spatial, w_temporal):
    middle = w_spatial.shape[2]
    return jnp.concatenate(
        [w_spatial.reshape(-1, middle), w_temporal.transpose(2, 0, 1).reshape(-1, middle)], axis=0
    )


def channel_dims():
    return (
        lax.axis_size("xhi"),
        lax.axis_size("zhi") * lax.axis_size("zlo"),
        lax.axis_size("xlo"),
        lax.axis_size("core"),
    )


def to_gathered_order(cells, block):
    lead = cells.shape[:-1]
    n = len(lead)
    split = cells.reshape(lead + channel_dims() + (block,))
    order = tuple(range(n)) + (n + 3, n, n + 2, n + 1, n + 4)
    return split.transpose(order).reshape(lead + (-1, block))


def from_gathered_order(cells, block):
    lead = cells.shape[:-1]
    n = len(lead)
    xhi, z, xlo, core = channel_dims()
    split = cells.reshape(lead + (core, xhi, xlo, z, block))
    order = tuple(range(n)) + (n + 1, n + 3, n + 2, n, n + 4)
    return split.transpose(order).reshape(lead + (-1,))


def shards(clip_tokens, w_spatial, w_temporal, frame_time, dilation):
    rows_dev, cols_dev, channels = clip_tokens.shape
    middle = w_spatial.shape[2]
    block_in = w_spatial.shape[1]
    block_out = w_temporal.shape[2]
    spatial_rows = w_spatial.shape[0] * block_in
    along_z = lax.all_gather(weight_rows(w_spatial, w_temporal), ("zhi", "zlo"), axis=0)
    values = clip_tokens.astype(jnp.float32)
    average = jnp.mean(values, axis=-1, keepdims=True)
    kernel_extent = jnp.mean(jnp.square(values - average), axis=-1, keepdims=True)
    normed = ((values - average) * lax.rsqrt(kernel_extent + 1e-06)).astype(jnp.bfloat16)
    normed = to_gathered_order(normed, block_in).reshape(rows_dev, cols_dev, channels)
    widened = padded_2(normed, ((FS, 1),), 1)
    blank_row = jnp.zeros((1,) + widened.shape[1:], jnp.bfloat16)
    lower_half = lax.axis_index(ST) % 2 == 1
    outgoing = jnp.where(lower_half, widened[:1], widened[-1:])
    incoming = partner(outgoing, ST, 0)
    top_rim = jnp.where(lower_half, incoming, blank_row)
    bottom_rim = jnp.where(lower_half, blank_row, incoming)
    padded = jnp.concatenate([top_rim, widened, bottom_rim], axis=0)
    first_row = lax.axis_index(ST) * rows_dev
    in_frame = (first_row + jnp.arange(rows_dev, dtype=jnp.int32)) % ROWS
    windows = []
    for shift_amount in (-1, 0, 1):
        inside = ((in_frame + shift_amount >= 0) & (in_frame + shift_amount < ROWS)).astype(
            jnp.bfloat16
        )
        windows.append(
            padded[1 + shift_amount : 1 + shift_amount + rows_dev] * inside[:, None, None]
        )
    tokens = rows_dev * cols_dev
    patches = []
    for row_tap in range(3):
        for column_kernel_tap in range(3):
            window = windows[row_tap][:, column_kernel_tap : column_kernel_tap + cols_dev, :]
            patches.append(window.reshape(tokens, -1, block_in))
    early = 3
    along_z, *head = lax.optimization_barrier((along_z, *patches[:early]))
    patches[:early] = head
    whole = lax.all_gather(along_z, ("xhi", "xlo"), axis=0)
    whole = lax.all_gather(whole, "core", axis=0)
    whole = whole.reshape((-1,) + along_z.shape[1:])
    running = jnp.zeros((tokens, middle), jnp.float32)
    for tap, patch in enumerate(patches):
        running = running + lax.dot_general(
            patch,
            whole[:, tap * block_in : (tap + 1) * block_in, :],
            (((1, 2), (0, 1)), ((), ())),
            preferred_element_type=jnp.float32,
        )
    hidden = jax.nn.gelu(running).astype(jnp.bfloat16)
    group_size = lax.axis_size(FRAME_AXES)
    per_pixel = tokens // group_size
    arrived = lax.all_to_all(
        hidden.reshape(group_size, per_pixel, middle), FRAME_AXES, 0, 0, tiled=True
    )
    group_width = middle // DGROUPS
    frame_sequence = arrived.reshape(FRAMES, per_pixel, DGROUPS, group_width)
    offsets = (jnp.arange(3, dtype=jnp.int32) - 1)[None, :] * dilation[:, None]
    selector_matrix = (
        frame_time[None, None, None, :]
        == frame_time[None, None, :, None] + offsets[:, :, None, None]
    ).astype(jnp.bfloat16)
    stacked_panels = jnp.einsum(
        "gkfe,epgc->fpkgc", selector_matrix, frame_sequence, preferred_element_type=jnp.float32
    )
    stacked_panels = stacked_panels.astype(jnp.bfloat16).reshape(FRAMES * per_pixel, 3, middle)
    xhi, z, xlo, core = channel_dims()
    temporal_w = whole[:, spatial_rows:, :].reshape(core, xhi, xlo, z, block_out, 3, middle)
    temporal_w = temporal_w.transpose(1, 3, 2, 0, 4, 5, 6).reshape(channels, 3, middle)
    result = lax.dot_general(
        stacked_panels, temporal_w, (((1, 2), (1, 2)), ((), ())), preferred_element_type=jnp.float32
    )
    mixed_out = result.astype(jnp.bfloat16)
    returned = lax.all_to_all(
        mixed_out.reshape(group_size, per_pixel, channels), FRAME_AXES, 0, 0, tiled=True
    )
    update = returned.reshape(rows_dev, cols_dev, channels)
    return (values + update.astype(jnp.float32)).astype(jnp.bfloat16)


def solution(mesh):
    clips = mesh.shape["clip"]
    fine = jax.sharding.Mesh(
        mesh.devices.reshape(clips, 2, -1, 2, 2, 2), ("clip",) + ALL
    )
    return jax.shard_map(
        shards,
        mesh=fine,
        in_specs=(
            P(("clip",) + ST, FS, None),
            P(None, ALL, None),
            P(None, None, ALL),
            P("clip"),
            P("clip"),
        ),
        out_specs=P(("clip",) + ST, FS, None),
        check_vma=False,
    )
```

```python
import jax
import jax.numpy as jnp
from jax import lax
from jax.sharding import PartitionSpec as P

DGROUPS = 8
FRAMES = 16
ROWS = 16
ST = ("xhi", "zhi", "zlo")
FS = ("xlo", "core")
FRAME_AXES = ("xhi", "zhi")
ALL = ("xhi", "zhi", "zlo", "xlo", "core")


def padded_2(cells, sides, width):
    for axis, dim in sides:
        count = lax.axis_size(axis)
        ends = count - 1
        head = lax.slice_in_dim(cells, 0, width, axis=dim)
        tail = lax.slice_in_dim(cells, cells.shape[dim] - width, cells.shape[dim], axis=dim)
        cells = jnp.concatenate(
            [
                lax.ppermute(tail, axis, [(i, (i + 1) % count) for i in range(ends)]),
                cells,
                lax.ppermute(head, axis, [((i + 1) % count, i) for i in range(ends)]),
            ],
            axis=dim,
        )
    return cells


def partner(value, axis, distance):
    mask = 2**distance
    pairs = [(source, source ^ mask) for source in range(lax.axis_size(axis))]
    return lax.ppermute(value, axis, pairs)


def weight_rows(w_spatial, w_temporal):
    middle = w_spatial.shape[2]
    return jnp.concatenate(
        [w_spatial.reshape(-1, middle), w_temporal.transpose(2, 0, 1).reshape(-1, middle)], axis=0
    )


def ring_gather(block, axis):
    count = lax.axis_size(axis)
    assert count == 4
    up = [(i, (i + 1) % count) for i in range(count)]
    down = [(i, (i - 1) % count) for i in range(count)]
    from_below = lax.ppermute(block, axis, up)
    from_above = lax.ppermute(block, axis, down)
    half = block.shape[1] // 2
    far_low = lax.ppermute(from_below[:, :half], axis, up)
    far_high = lax.ppermute(from_above[:, half:], axis, down)
    far = jnp.concatenate([far_low, far_high], axis=1)
    by_offset = jnp.stack([block, from_above, far, from_below])
    me = lax.axis_index(axis)
    doubled = jnp.concatenate([by_offset, by_offset])
    return lax.dynamic_slice_in_dim(doubled, count - me, count, axis=0)


def channel_dims():
    return (
        lax.axis_size("xhi"),
        lax.axis_size("zhi") * lax.axis_size("zlo"),
        lax.axis_size("xlo"),
        lax.axis_size("core"),
    )


def to_gathered_order(cells, block):
    lead = cells.shape[:-1]
    n = len(lead)
    split = cells.reshape(lead + channel_dims() + (block,))
    order = tuple(range(n)) + (n + 3, n, n + 2, n + 1, n + 4)
    return split.transpose(order).reshape(lead + (-1, block))


def from_gathered_order(cells, block):
    lead = cells.shape[:-1]
    n = len(lead)
    xhi, z, xlo, core = channel_dims()
    split = cells.reshape(lead + (core, xhi, xlo, z, block))
    order = tuple(range(n)) + (n + 1, n + 3, n + 2, n, n + 4)
    return split.transpose(order).reshape(lead + (-1,))


def shards(clip_tokens, w_spatial, w_temporal, frame_time, dilation):
    rows_dev, cols_dev, channels = clip_tokens.shape
    middle = w_spatial.shape[2]
    block_in = w_spatial.shape[1]
    block_out = w_temporal.shape[2]
    spatial_rows = w_spatial.shape[0] * block_in
    along_z = lax.all_gather(weight_rows(w_spatial, w_temporal), ("zhi", "zlo"), axis=0)
    values = clip_tokens.astype(jnp.float32)
    average = jnp.mean(values, axis=-1, keepdims=True)
    kernel_extent = jnp.mean(jnp.square(values - average), axis=-1, keepdims=True)
    normed = ((values - average) * lax.rsqrt(kernel_extent + 1e-06)).astype(jnp.bfloat16)
    normed = to_gathered_order(normed, block_in).reshape(rows_dev, cols_dev, channels)
    widened = padded_2(normed, ((FS, 1),), 1)
    blank_row = jnp.zeros((1,) + widened.shape[1:], jnp.bfloat16)
    lower_half = lax.axis_index(ST) % 2 == 1
    outgoing = jnp.where(lower_half, widened[:1], widened[-1:])
    incoming = partner(outgoing, ST, 0)
    top_rim = jnp.where(lower_half, incoming, blank_row)
    bottom_rim = jnp.where(lower_half, blank_row, incoming)
    padded = jnp.concatenate([top_rim, widened, bottom_rim], axis=0)
    first_row = lax.axis_index(ST) * rows_dev
    in_frame = (first_row + jnp.arange(rows_dev, dtype=jnp.int32)) % ROWS
    windows = []
    for shift_amount in (-1, 0, 1):
        inside = ((in_frame + shift_amount >= 0) & (in_frame + shift_amount < ROWS)).astype(
            jnp.bfloat16
        )
        windows.append(
            padded[1 + shift_amount : 1 + shift_amount + rows_dev] * inside[:, None, None]
        )
    tokens = rows_dev * cols_dev
    patches = []
    for row_tap in range(3):
        for column_kernel_tap in range(3):
            window = windows[row_tap][:, column_kernel_tap : column_kernel_tap + cols_dev, :]
            patches.append(window.reshape(tokens, -1, block_in))
    early = 3
    along_z, *head = lax.optimization_barrier((along_z, *patches[:early]))
    patches[:early] = head
    split = along_z.shape[1] // 2
    first = lax.all_gather(along_z[:, :split], ("xhi", "xlo"), axis=0)
    second = ring_gather(along_z[:, split:], ("xhi", "xlo"))
    halves = []
    for part in (first, second):
        part = lax.all_gather(part, "core", axis=0)
        halves.append(part.reshape((-1,) + part.shape[3:]))
    running = jnp.zeros((tokens, middle), jnp.float32)
    for tap, patch in enumerate(patches):
        row = tap * block_in
        running = running + lax.dot_general(
            patch,
            halves[row // split][:, row % split : row % split + block_in, :],
            (((1, 2), (0, 1)), ((), ())),
            preferred_element_type=jnp.float32,
        )
    hidden = jax.nn.gelu(running).astype(jnp.bfloat16)
    group_size = lax.axis_size(FRAME_AXES)
    per_pixel = tokens // group_size
    arrived = lax.all_to_all(
        hidden.reshape(group_size, per_pixel, middle), FRAME_AXES, 0, 0, tiled=True
    )
    group_width = middle // DGROUPS
    frame_sequence = arrived.reshape(FRAMES, per_pixel, DGROUPS, group_width)
    offsets = (jnp.arange(3, dtype=jnp.int32) - 1)[None, :] * dilation[:, None]
    selector_matrix = (
        frame_time[None, None, None, :]
        == frame_time[None, None, :, None] + offsets[:, :, None, None]
    ).astype(jnp.bfloat16)
    stacked_panels = jnp.einsum(
        "gkfe,epgc->fpkgc", selector_matrix, frame_sequence, preferred_element_type=jnp.float32
    )
    stacked_panels = stacked_panels.astype(jnp.bfloat16).reshape(FRAMES * per_pixel, 3, middle)
    xhi, z, xlo, core = channel_dims()
    temporal_w = halves[1][:, spatial_rows - split :, :].reshape(core, xhi, xlo, z, block_out, 3, middle)
    temporal_w = temporal_w.transpose(1, 3, 2, 0, 4, 5, 6).reshape(channels, 3, middle)
    result = lax.dot_general(
        stacked_panels, temporal_w, (((1, 2), (1, 2)), ((), ())), preferred_element_type=jnp.float32
    )
    mixed_out = result.astype(jnp.bfloat16)
    returned = lax.all_to_all(
        mixed_out.reshape(group_size, per_pixel, channels), FRAME_AXES, 0, 0, tiled=True
    )
    update = returned.reshape(rows_dev, cols_dev, channels)
    return (values + update.astype(jnp.float32)).astype(jnp.bfloat16)


def solution(mesh):
    clips = mesh.shape["clip"]
    fine = jax.sharding.Mesh(
        mesh.devices.reshape(clips, 2, -1, 2, 2, 2), ("clip",) + ALL
    )
    return jax.shard_map(
        shards,
        mesh=fine,
        in_specs=(
            P(("clip",) + ST, FS, None),
            P(None, ALL, None),
            P(None, None, ALL),
            P("clip"),
            P("clip"),
        ),
        out_specs=P(("clip",) + ST, FS, None),
        check_vma=False,
    )
```

```python
import jax
import jax.numpy as jnp
from jax import lax
from jax.sharding import PartitionSpec as P

DGROUPS = 8
FRAMES = 16
ROWS = 16
ST = ("xhi", "zhi", "zlo")
FS = ("xlo", "core")
FRAME_AXES = ("xhi", "zhi")
ALL = ("xhi", "zhi", "zlo", "xlo", "core")


def padded_2(cells, sides, width):
    for axis, dim in sides:
        count = lax.axis_size(axis)
        ends = count - 1
        head = lax.slice_in_dim(cells, 0, width, axis=dim)
        tail = lax.slice_in_dim(cells, cells.shape[dim] - width, cells.shape[dim], axis=dim)
        cells = jnp.concatenate(
            [
                lax.ppermute(tail, axis, [(i, (i + 1) % count) for i in range(ends)]),
                cells,
                lax.ppermute(head, axis, [((i + 1) % count, i) for i in range(ends)]),
            ],
            axis=dim,
        )
    return cells


def partner(value, axis, distance):
    mask = 2**distance
    pairs = [(source, source ^ mask) for source in range(lax.axis_size(axis))]
    return lax.ppermute(value, axis, pairs)


def weight_rows(w_spatial, w_temporal):
    middle = w_spatial.shape[2]
    return jnp.concatenate(
        [w_spatial.reshape(-1, middle), w_temporal.transpose(2, 0, 1).reshape(-1, middle)], axis=0
    )


def channel_dims():
    return (
        lax.axis_size("xhi"),
        lax.axis_size("zhi") * lax.axis_size("zlo"),
        lax.axis_size("xlo"),
        lax.axis_size("core"),
    )


def to_gathered_order(cells, block):
    lead = cells.shape[:-1]
    n = len(lead)
    split = cells.reshape(lead + channel_dims() + (block,))
    order = tuple(range(n)) + (n + 3, n, n + 2, n + 1, n + 4)
    return split.transpose(order).reshape(lead + (-1, block))


def from_gathered_order(cells, block):
    lead = cells.shape[:-1]
    n = len(lead)
    xhi, z, xlo, core = channel_dims()
    split = cells.reshape(lead + (core, xhi, xlo, z, block))
    order = tuple(range(n)) + (n + 1, n + 3, n + 2, n, n + 4)
    return split.transpose(order).reshape(lead + (-1,))


def shards(clip_tokens, w_spatial, w_temporal, frame_time, dilation):
    rows_dev, cols_dev, channels = clip_tokens.shape
    middle = w_spatial.shape[2]
    block_in = w_spatial.shape[1]
    block_out = w_temporal.shape[2]
    spatial_rows = w_spatial.shape[0] * block_in
    along_z = lax.all_gather(weight_rows(w_spatial, w_temporal), ("zhi", "zlo"), axis=0)
    values = clip_tokens.astype(jnp.float32)
    average = jnp.mean(values, axis=-1, keepdims=True)
    kernel_extent = jnp.mean(jnp.square(values - average), axis=-1, keepdims=True)
    normed = ((values - average) * lax.rsqrt(kernel_extent + 1e-06)).astype(jnp.bfloat16)
    normed = to_gathered_order(normed, block_in).reshape(rows_dev, cols_dev, channels)
    widened = padded_2(normed, ((FS, 1),), 1)
    blank_row = jnp.zeros((1,) + widened.shape[1:], jnp.bfloat16)
    lower_half = lax.axis_index(ST) % 2 == 1
    outgoing = jnp.where(lower_half, widened[:1], widened[-1:])
    incoming = partner(outgoing, ST, 0)
    top_rim = jnp.where(lower_half, incoming, blank_row)
    bottom_rim = jnp.where(lower_half, blank_row, incoming)
    padded = jnp.concatenate([top_rim, widened, bottom_rim], axis=0)
    first_row = lax.axis_index(ST) * rows_dev
    in_frame = (first_row + jnp.arange(rows_dev, dtype=jnp.int32)) % ROWS
    masks = []
    for shift_amount in (-1, 0, 1):
        masks.append(
            ((in_frame + shift_amount >= 0) & (in_frame + shift_amount < ROWS)).astype(jnp.bfloat16)
        )
    tokens = rows_dev * cols_dev
    other_core = [(0, 1), (1, 0)]
    partner_padded = lax.ppermute(padded, "core", other_core)
    half_blocks = channels // block_in // lax.axis_size("core")
    start = lax.axis_index("core") * half_blocks
    width = half_blocks * block_in
    own_part = lax.dynamic_slice_in_dim(padded, start * block_in, width, axis=2)
    partner_part = lax.dynamic_slice_in_dim(partner_padded, start * block_in, width, axis=2)
    patches = []
    for row_tap in range(3):
        inside = masks[row_tap][:, None, None]
        mine = own_part[row_tap : row_tap + rows_dev] * inside
        theirs = partner_part[row_tap : row_tap + rows_dev] * inside
        for column_kernel_tap in range(3):
            both = jnp.concatenate(
                [
                    src_tile[:, column_kernel_tap : column_kernel_tap + cols_dev, :]
                    for src_tile in (mine, theirs)
                ]
            )
            patches.append(both.reshape(2 * tokens, -1, block_in))
    early = 3
    along_z, *head = lax.optimization_barrier((along_z, *patches[:early]))
    patches[:early] = head
    own_half = lax.all_gather(along_z, ("xhi", "xlo"), axis=0)
    own_half = own_half.reshape((-1,) + along_z.shape[1:])
    partial = jnp.zeros((2 * tokens, middle), jnp.float32)
    for tap, patch in enumerate(patches):
        partial = partial + lax.dot_general(
            patch,
            own_half[:, tap * block_in : (tap + 1) * block_in, :],
            (((1, 2), (0, 1)), ((), ())),
            preferred_element_type=jnp.float32,
        )
    running = partial[:tokens] + lax.ppermute(partial[tokens:], "core", other_core)
    hidden = jax.nn.gelu(running).astype(jnp.bfloat16)
    group_size = lax.axis_size(FRAME_AXES)
    per_pixel = tokens // group_size
    arrived = lax.all_to_all(
        hidden.reshape(group_size, per_pixel, middle), FRAME_AXES, 0, 0, tiled=True
    )
    group_width = middle // DGROUPS
    frame_sequence = arrived.reshape(FRAMES, per_pixel, DGROUPS, group_width)
    offsets = (jnp.arange(3, dtype=jnp.int32) - 1)[None, :] * dilation[:, None]
    selector_matrix = (
        frame_time[None, None, None, :]
        == frame_time[None, None, :, None] + offsets[:, :, None, None]
    ).astype(jnp.bfloat16)
    stacked_panels = jnp.einsum(
        "gkfe,epgc->fpkgc", selector_matrix, frame_sequence, preferred_element_type=jnp.float32
    )
    stacked_panels = stacked_panels.astype(jnp.bfloat16).reshape(FRAMES * per_pixel, 3, middle)
    xhi, z, xlo, core = channel_dims()
    temporal_w = lax.all_gather(own_half[:, spatial_rows:, :], "core", axis=0)
    temporal_w = temporal_w.reshape(core, xhi, xlo, z, block_out, 3, middle)
    temporal_w = temporal_w.transpose(1, 3, 2, 0, 4, 5, 6).reshape(channels, 3, middle)
    result = lax.dot_general(
        stacked_panels, temporal_w, (((1, 2), (1, 2)), ((), ())), preferred_element_type=jnp.float32
    )
    mixed_out = result.astype(jnp.bfloat16)
    returned = lax.all_to_all(
        mixed_out.reshape(group_size, per_pixel, channels), FRAME_AXES, 0, 0, tiled=True
    )
    update = returned.reshape(rows_dev, cols_dev, channels)
    return (values + update.astype(jnp.float32)).astype(jnp.bfloat16)


def solution(mesh):
    clips = mesh.shape["clip"]
    fine = jax.sharding.Mesh(
        mesh.devices.reshape(clips, 2, -1, 2, 2, 2), ("clip",) + ALL
    )
    return jax.shard_map(
        shards,
        mesh=fine,
        in_specs=(
            P(("clip",) + ST, FS, None),
            P(None, ALL, None),
            P(None, None, ALL),
            P("clip"),
            P("clip"),
        ),
        out_specs=P(("clip",) + ST, FS, None),
        check_vma=False,
    )
```

```python
import jax
import jax.numpy as jnp
from jax import lax
from jax.sharding import PartitionSpec as P

DGROUPS = 8
FRAMES = 16
ROWS = 16
ST = ("xhi", "zhi", "zlo")
FS = ("xlo", "core")
FRAME_AXES = ("xhi", "zhi")
ALL = ("xhi", "zhi", "zlo", "xlo", "core")


def padded_2(cells, sides, width):
    for axis, dim in sides:
        count = lax.axis_size(axis)
        ends = count - 1
        head = lax.slice_in_dim(cells, 0, width, axis=dim)
        tail = lax.slice_in_dim(cells, cells.shape[dim] - width, cells.shape[dim], axis=dim)
        cells = jnp.concatenate(
            [
                lax.ppermute(tail, axis, [(i, (i + 1) % count) for i in range(ends)]),
                cells,
                lax.ppermute(head, axis, [((i + 1) % count, i) for i in range(ends)]),
            ],
            axis=dim,
        )
    return cells


def partner(value, axis, distance):
    mask = 2**distance
    pairs = [(source, source ^ mask) for source in range(lax.axis_size(axis))]
    return lax.ppermute(value, axis, pairs)


def weight_rows(w_spatial, w_temporal):
    middle = w_spatial.shape[2]
    return jnp.concatenate(
        [w_spatial.reshape(-1, middle), w_temporal.transpose(2, 0, 1).reshape(-1, middle)], axis=0
    )


def ring_gather(block, axis):
    count = lax.axis_size(axis)
    assert count == 4
    up = [(i, (i + 1) % count) for i in range(count)]
    down = [(i, (i - 1) % count) for i in range(count)]
    from_below = lax.ppermute(block, axis, up)
    from_above = lax.ppermute(block, axis, down)
    half = block.shape[1] // 2
    far_low = lax.ppermute(from_below[:, :half], axis, up)
    far_high = lax.ppermute(from_above[:, half:], axis, down)
    far = jnp.concatenate([far_low, far_high], axis=1)
    return jnp.stack([block, from_above, far, from_below])


def channel_dims():
    return (
        lax.axis_size("xhi"),
        lax.axis_size("zhi") * lax.axis_size("zlo"),
        lax.axis_size("xlo"),
        lax.axis_size("core"),
    )


def to_gathered_order(cells, block):
    lead = cells.shape[:-1]
    n = len(lead)
    split = cells.reshape(lead + channel_dims() + (block,))
    order = tuple(range(n)) + (n + 3, n, n + 2, n + 1, n + 4)
    return split.transpose(order).reshape(lead + (-1, block))


def from_gathered_order(cells, block):
    lead = cells.shape[:-1]
    n = len(lead)
    xhi, z, xlo, core = channel_dims()
    split = cells.reshape(lead + (core, xhi, xlo, z, block))
    order = tuple(range(n)) + (n + 1, n + 3, n + 2, n, n + 4)
    return split.transpose(order).reshape(lead + (-1,))


def shards(clip_tokens, w_spatial, w_temporal, frame_time, dilation):
    rows_dev, cols_dev, channels = clip_tokens.shape
    middle = w_spatial.shape[2]
    block_in = w_spatial.shape[1]
    block_out = w_temporal.shape[2]
    spatial_rows = w_spatial.shape[0] * block_in
    along_z = lax.all_gather(weight_rows(w_spatial, w_temporal), ("zhi", "zlo"), axis=0)
    values = clip_tokens.astype(jnp.float32)
    average = jnp.mean(values, axis=-1, keepdims=True)
    kernel_extent = jnp.mean(jnp.square(values - average), axis=-1, keepdims=True)
    normed = ((values - average) * lax.rsqrt(kernel_extent + 1e-06)).astype(jnp.bfloat16)
    normed = to_gathered_order(normed, block_in).reshape(rows_dev, cols_dev, channels)
    widened = padded_2(normed, ((FS, 1),), 1)
    blank_row = jnp.zeros((1,) + widened.shape[1:], jnp.bfloat16)
    lower_half = lax.axis_index(ST) % 2 == 1
    outgoing = jnp.where(lower_half, widened[:1], widened[-1:])
    incoming = partner(outgoing, ST, 0)
    top_rim = jnp.where(lower_half, incoming, blank_row)
    bottom_rim = jnp.where(lower_half, blank_row, incoming)
    padded = jnp.concatenate([top_rim, widened, bottom_rim], axis=0)
    first_row = lax.axis_index(ST) * rows_dev
    in_frame = (first_row + jnp.arange(rows_dev, dtype=jnp.int32)) % ROWS
    masks = []
    for shift_amount in (-1, 0, 1):
        masks.append(
            ((in_frame + shift_amount >= 0) & (in_frame + shift_amount < ROWS)).astype(jnp.bfloat16)
        )
    tokens = rows_dev * cols_dev
    other_core = [(0, 1), (1, 0)]
    partner_padded = lax.ppermute(padded, "core", other_core)
    half_blocks = channels // block_in // lax.axis_size("core")
    start = lax.axis_index("core") * half_blocks
    width = half_blocks * block_in
    me_x = lax.axis_index(("xhi", "xlo"))
    n_x = lax.axis_size(("xhi", "xlo"))
    own_part, partner_part = [
        jnp.roll(
            lax.dynamic_slice_in_dim(part, start * block_in, width, axis=2).reshape(
                part.shape[:2] + (n_x, -1)
            ),
            -me_x,
            axis=2,
        ).reshape(part.shape[:2] + (width,))
        for part in (padded, partner_padded)
    ]
    patches = []
    for row_tap in range(3):
        inside = masks[row_tap][:, None, None]
        mine = own_part[row_tap : row_tap + rows_dev] * inside
        theirs = partner_part[row_tap : row_tap + rows_dev] * inside
        for column_kernel_tap in range(3):
            both = jnp.concatenate(
                [
                    src_tile[:, column_kernel_tap : column_kernel_tap + cols_dev, :]
                    for src_tile in (mine, theirs)
                ]
            )
            patches.append(both.reshape(2 * tokens, -1, block_in))
    early = 3
    along_z, *head = lax.optimization_barrier((along_z, *patches[:early]))
    patches[:early] = head
    own_half = ring_gather(along_z, ("xhi", "xlo"))
    own_half = own_half.reshape((-1,) + along_z.shape[1:])
    partial = jnp.zeros((2 * tokens, middle), jnp.float32)
    for tap, patch in enumerate(patches):
        partial = partial + lax.dot_general(
            patch,
            own_half[:, tap * block_in : (tap + 1) * block_in, :],
            (((1, 2), (0, 1)), ((), ())),
            preferred_element_type=jnp.float32,
        )
    running = partial[:tokens] + lax.ppermute(partial[tokens:], "core", other_core)
    hidden = jax.nn.gelu(running).astype(jnp.bfloat16)
    group_size = lax.axis_size(FRAME_AXES)
    per_pixel = tokens // group_size
    arrived = lax.all_to_all(
        hidden.reshape(group_size, per_pixel, middle), FRAME_AXES, 0, 0, tiled=True
    )
    group_width = middle // DGROUPS
    frame_sequence = arrived.reshape(FRAMES, per_pixel, DGROUPS, group_width)
    offsets = (jnp.arange(3, dtype=jnp.int32) - 1)[None, :] * dilation[:, None]
    selector_matrix = (
        frame_time[None, None, None, :]
        == frame_time[None, None, :, None] + offsets[:, :, None, None]
    ).astype(jnp.bfloat16)
    stacked_panels = jnp.einsum(
        "gkfe,epgc->fpkgc", selector_matrix, frame_sequence, preferred_element_type=jnp.float32
    )
    stacked_panels = stacked_panels.astype(jnp.bfloat16).reshape(FRAMES * per_pixel, 3, middle)
    xhi, z, xlo, core = channel_dims()
    temporal_w = lax.all_gather(own_half[:, spatial_rows:, :], "core", axis=0)
    temporal_w = jnp.roll(temporal_w.reshape((core, xhi * xlo, -1) + temporal_w.shape[2:]), me_x, axis=1)
    temporal_w = temporal_w.reshape(core, xhi, xlo, z, block_out, 3, middle)
    temporal_w = temporal_w.transpose(1, 3, 2, 0, 4, 5, 6).reshape(channels, 3, middle)
    result = lax.dot_general(
        stacked_panels, temporal_w, (((1, 2), (1, 2)), ((), ())), preferred_element_type=jnp.float32
    )
    mixed_out = result.astype(jnp.bfloat16)
    returned = lax.all_to_all(
        mixed_out.reshape(group_size, per_pixel, channels), FRAME_AXES, 0, 0, tiled=True
    )
    update = returned.reshape(rows_dev, cols_dev, channels)
    return (values + update.astype(jnp.float32)).astype(jnp.bfloat16)


def solution(mesh):
    clips = mesh.shape["clip"]
    fine = jax.sharding.Mesh(
        mesh.devices.reshape(clips, 2, -1, 2, 2, 2), ("clip",) + ALL
    )
    return jax.shard_map(
        shards,
        mesh=fine,
        in_specs=(
            P(("clip",) + ST, FS, None),
            P(None, ALL, None),
            P(None, None, ALL),
            P("clip"),
            P("clip"),
        ),
        out_specs=P(("clip",) + ST, FS, None),
        check_vma=False,
    )
```

```python
import jax
import jax.numpy as jnp
from jax import lax
from jax.sharding import PartitionSpec as P

DGROUPS = 8
FRAMES = 16
ROWS = 16
ST = ("xhi", "zhi", "zlo")
FS = ("xlo", "core")
FRAME_AXES = ("xhi", "zhi")
ALL = ("xhi", "zhi", "zlo", "xlo", "core")


def padded_2(cells, sides, width):
    for axis, dim in sides:
        count = lax.axis_size(axis)
        ends = count - 1
        head = lax.slice_in_dim(cells, 0, width, axis=dim)
        tail = lax.slice_in_dim(cells, cells.shape[dim] - width, cells.shape[dim], axis=dim)
        cells = jnp.concatenate(
            [
                lax.ppermute(tail, axis, [(i, (i + 1) % count) for i in range(ends)]),
                cells,
                lax.ppermute(head, axis, [((i + 1) % count, i) for i in range(ends)]),
            ],
            axis=dim,
        )
    return cells


def partner(value, axis, distance):
    mask = 2**distance
    pairs = [(source, source ^ mask) for source in range(lax.axis_size(axis))]
    return lax.ppermute(value, axis, pairs)


def weight_rows(w_spatial, w_temporal):
    middle = w_spatial.shape[2]
    return jnp.concatenate(
        [w_spatial.reshape(-1, middle), w_temporal.transpose(2, 0, 1).reshape(-1, middle)], axis=0
    )


def channel_dims():
    return (
        lax.axis_size("xhi"),
        lax.axis_size("zhi") * lax.axis_size("zlo"),
        lax.axis_size("xlo"),
        lax.axis_size("core"),
    )


def to_gathered_order(cells, block):
    lead = cells.shape[:-1]
    n = len(lead)
    split = cells.reshape(lead + channel_dims() + (block,))
    order = tuple(range(n)) + (n + 3, n, n + 2, n + 1, n + 4)
    return split.transpose(order).reshape(lead + (-1, block))


def from_gathered_order(cells, block):
    lead = cells.shape[:-1]
    n = len(lead)
    xhi, z, xlo, core = channel_dims()
    split = cells.reshape(lead + (core, xhi, xlo, z, block))
    order = tuple(range(n)) + (n + 1, n + 3, n + 2, n, n + 4)
    return split.transpose(order).reshape(lead + (-1,))


def shards(clip_tokens, w_spatial, w_temporal, frame_time, dilation):
    rows_dev, cols_dev, channels = clip_tokens.shape
    middle = w_spatial.shape[2]
    block_in = w_spatial.shape[1]
    block_out = w_temporal.shape[2]
    spatial_rows = w_spatial.shape[0] * block_in
    along_z = lax.all_gather(weight_rows(w_spatial, w_temporal), ("zhi", "zlo"), axis=0)
    values = clip_tokens.astype(jnp.float32)
    average = jnp.mean(values, axis=-1, keepdims=True)
    kernel_extent = jnp.mean(jnp.square(values - average), axis=-1, keepdims=True)
    normed = ((values - average) * lax.rsqrt(kernel_extent + 1e-06)).astype(jnp.bfloat16)
    normed = to_gathered_order(normed, block_in).reshape(rows_dev, cols_dev, channels)
    widened = padded_2(normed, ((FS, 1),), 1)
    blank_row = jnp.zeros((1,) + widened.shape[1:], jnp.bfloat16)
    lower_half = lax.axis_index(ST) % 2 == 1
    outgoing = jnp.where(lower_half, widened[:1], widened[-1:])
    incoming = partner(outgoing, ST, 0)
    top_rim = jnp.where(lower_half, incoming, blank_row)
    bottom_rim = jnp.where(lower_half, blank_row, incoming)
    padded = jnp.concatenate([top_rim, widened, bottom_rim], axis=0)
    first_row = lax.axis_index(ST) * rows_dev
    in_frame = (first_row + jnp.arange(rows_dev, dtype=jnp.int32)) % ROWS
    masks = []
    for shift_amount in (-1, 0, 1):
        masks.append(
            ((in_frame + shift_amount >= 0) & (in_frame + shift_amount < ROWS)).astype(jnp.bfloat16)
        )
    tokens = rows_dev * cols_dev
    other_core = [(0, 1), (1, 0)]
    partner_padded = lax.ppermute(padded, "core", other_core)
    half_blocks = channels // block_in // lax.axis_size("core")
    start = lax.axis_index("core") * half_blocks
    width = half_blocks * block_in
    own_part = lax.dynamic_slice_in_dim(padded, start * block_in, width, axis=2)
    partner_part = lax.dynamic_slice_in_dim(partner_padded, start * block_in, width, axis=2)
    patches = []
    for row_tap in range(3):
        inside = masks[row_tap][:, None, None]
        mine = own_part[row_tap : row_tap + rows_dev] * inside
        theirs = partner_part[row_tap : row_tap + rows_dev] * inside
        for column_kernel_tap in range(3):
            both = jnp.concatenate(
                [
                    src_tile[:, column_kernel_tap : column_kernel_tap + cols_dev, :]
                    for src_tile in (mine, theirs)
                ]
            )
            patches.append(both.reshape(2 * tokens, -1, block_in))
    early = 3
    along_z, *head = lax.optimization_barrier((along_z, *patches[:early]))
    patches[:early] = head
    own_half = lax.all_gather(along_z[:, :spatial_rows], ("xhi", "xlo"), axis=0)
    own_half = own_half.reshape((-1, spatial_rows) + along_z.shape[2:])
    own_half, temporal_rows = lax.optimization_barrier((own_half, along_z[:, spatial_rows:]))
    temporal_rows = lax.all_gather(temporal_rows, ("xhi", "xlo"), axis=0)
    partial = jnp.zeros((2 * tokens, middle), jnp.float32)
    for tap, patch in enumerate(patches):
        partial = partial + lax.dot_general(
            patch,
            own_half[:, tap * block_in : (tap + 1) * block_in, :],
            (((1, 2), (0, 1)), ((), ())),
            preferred_element_type=jnp.float32,
        )
    running = partial[:tokens] + lax.ppermute(partial[tokens:], "core", other_core)
    hidden = jax.nn.gelu(running).astype(jnp.bfloat16)
    group_size = lax.axis_size(FRAME_AXES)
    per_pixel = tokens // group_size
    arrived = lax.all_to_all(
        hidden.reshape(group_size, per_pixel, middle), FRAME_AXES, 0, 0, tiled=True
    )
    group_width = middle // DGROUPS
    frame_sequence = arrived.reshape(FRAMES, per_pixel, DGROUPS, group_width)
    offsets = (jnp.arange(3, dtype=jnp.int32) - 1)[None, :] * dilation[:, None]
    selector_matrix = (
        frame_time[None, None, None, :]
        == frame_time[None, None, :, None] + offsets[:, :, None, None]
    ).astype(jnp.bfloat16)
    stacked_panels = jnp.einsum(
        "gkfe,epgc->fpkgc", selector_matrix, frame_sequence, preferred_element_type=jnp.float32
    )
    stacked_panels = stacked_panels.astype(jnp.bfloat16).reshape(FRAMES * per_pixel, 3, middle)
    xhi, z, xlo, core = channel_dims()
    temporal_w = lax.all_gather(temporal_rows, "core", axis=0)
    temporal_w = temporal_w.reshape(core, xhi, xlo, z, block_out, 3, middle)
    temporal_w = temporal_w.transpose(1, 3, 2, 0, 4, 5, 6).reshape(channels, 3, middle)
    result = lax.dot_general(
        stacked_panels, temporal_w, (((1, 2), (1, 2)), ((), ())), preferred_element_type=jnp.float32
    )
    mixed_out = result.astype(jnp.bfloat16)
    returned = lax.all_to_all(
        mixed_out.reshape(group_size, per_pixel, channels), FRAME_AXES, 0, 0, tiled=True
    )
    update = returned.reshape(rows_dev, cols_dev, channels)
    return (values + update.astype(jnp.float32)).astype(jnp.bfloat16)


def solution(mesh):
    clips = mesh.shape["clip"]
    fine = jax.sharding.Mesh(
        mesh.devices.reshape(clips, 2, -1, 2, 2, 2), ("clip",) + ALL
    )
    return jax.shard_map(
        shards,
        mesh=fine,
        in_specs=(
            P(("clip",) + ST, FS, None),
            P(None, ALL, None),
            P(None, None, ALL),
            P("clip"),
            P("clip"),
        ),
        out_specs=P(("clip",) + ST, FS, None),
        check_vma=False,
    )
```

```python
import jax
import jax.numpy as jnp
from jax import lax
from jax.sharding import PartitionSpec as P

DGROUPS = 8
FRAMES = 16
ROWS = 16
ST = ("xhi", "zhi", "zlo")
FS = ("xlo", "core")
FRAME_AXES = ("xhi", "zhi")
ALL = ("xhi", "zhi", "zlo", "xlo", "core")


def padded_2(cells, sides, width):
    for axis, dim in sides:
        count = lax.axis_size(axis)
        ends = count - 1
        head = lax.slice_in_dim(cells, 0, width, axis=dim)
        tail = lax.slice_in_dim(cells, cells.shape[dim] - width, cells.shape[dim], axis=dim)
        cells = jnp.concatenate(
            [
                lax.ppermute(tail, axis, [(i, (i + 1) % count) for i in range(ends)]),
                cells,
                lax.ppermute(head, axis, [((i + 1) % count, i) for i in range(ends)]),
            ],
            axis=dim,
        )
    return cells


def partner(value, axis, distance):
    mask = 2**distance
    pairs = [(source, source ^ mask) for source in range(lax.axis_size(axis))]
    return lax.ppermute(value, axis, pairs)


def weight_rows(w_spatial, w_temporal):
    middle = w_spatial.shape[2]
    return jnp.concatenate(
        [w_spatial.reshape(-1, middle), w_temporal.transpose(2, 0, 1).reshape(-1, middle)], axis=0
    )


def channel_dims():
    return (
        lax.axis_size("xhi"),
        lax.axis_size("zhi") * lax.axis_size("zlo"),
        lax.axis_size("xlo"),
        lax.axis_size("core"),
    )


def to_gathered_order(cells, block):
    lead = cells.shape[:-1]
    n = len(lead)
    split = cells.reshape(lead + channel_dims() + (block,))
    order = tuple(range(n)) + (n + 3, n, n + 2, n + 1, n + 4)
    return split.transpose(order).reshape(lead + (-1, block))


def from_gathered_order(cells, block):
    lead = cells.shape[:-1]
    n = len(lead)
    xhi, z, xlo, core = channel_dims()
    split = cells.reshape(lead + (core, xhi, xlo, z, block))
    order = tuple(range(n)) + (n + 1, n + 3, n + 2, n, n + 4)
    return split.transpose(order).reshape(lead + (-1,))


def shards(clip_tokens, w_spatial, w_temporal, frame_time, dilation):
    rows_dev, cols_dev, channels = clip_tokens.shape
    middle = w_spatial.shape[2]
    block_in = w_spatial.shape[1]
    block_out = w_temporal.shape[2]
    spatial_rows = w_spatial.shape[0] * block_in
    along_z = lax.all_gather(weight_rows(w_spatial, w_temporal), ("zhi", "zlo"), axis=0)
    values = clip_tokens.astype(jnp.float32)
    average = jnp.mean(values, axis=-1, keepdims=True)
    kernel_extent = jnp.mean(jnp.square(values - average), axis=-1, keepdims=True)
    normed = ((values - average) * lax.rsqrt(kernel_extent + 1e-06)).astype(jnp.bfloat16)
    normed = to_gathered_order(normed, block_in).reshape(rows_dev, cols_dev, channels)
    widened = padded_2(normed, ((FS, 1),), 1)
    blank_row = jnp.zeros((1,) + widened.shape[1:], jnp.bfloat16)
    lower_half = lax.axis_index(ST) % 2 == 1
    outgoing = jnp.where(lower_half, widened[:1], widened[-1:])
    incoming = partner(outgoing, ST, 0)
    top_rim = jnp.where(lower_half, incoming, blank_row)
    bottom_rim = jnp.where(lower_half, blank_row, incoming)
    padded = jnp.concatenate([top_rim, widened, bottom_rim], axis=0)
    first_row = lax.axis_index(ST) * rows_dev
    in_frame = (first_row + jnp.arange(rows_dev, dtype=jnp.int32)) % ROWS
    masks = []
    for shift_amount in (-1, 0, 1):
        masks.append(
            ((in_frame + shift_amount >= 0) & (in_frame + shift_amount < ROWS)).astype(jnp.bfloat16)
        )
    tokens = rows_dev * cols_dev
    other_core = [(0, 1), (1, 0)]
    partner_padded = lax.ppermute(padded, "core", other_core)
    half_blocks = channels // block_in // lax.axis_size("core")
    start = lax.axis_index("core") * half_blocks
    width = half_blocks * block_in
    own_part = lax.dynamic_slice_in_dim(padded, start * block_in, width, axis=2)
    partner_part = lax.dynamic_slice_in_dim(partner_padded, start * block_in, width, axis=2)
    patches = []
    for row_tap in range(3):
        inside = masks[row_tap][:, None, None]
        mine = own_part[row_tap : row_tap + rows_dev] * inside
        theirs = partner_part[row_tap : row_tap + rows_dev] * inside
        for column_kernel_tap in range(3):
            both = jnp.concatenate(
                [
                    src_tile[:, column_kernel_tap : column_kernel_tap + cols_dev, :]
                    for src_tile in (mine, theirs)
                ]
            )
            patches.append(both.reshape(2 * tokens, -1, block_in))
    early = 3
    along_z, *head = lax.optimization_barrier((along_z, *patches[:early]))
    patches[:early] = head
    own_half = lax.all_gather(along_z[:, :spatial_rows], ("xhi", "xlo"), axis=0)
    own_half = own_half.reshape((-1, spatial_rows) + along_z.shape[2:])
    temporal_rows = along_z[:, spatial_rows:]
    partial = jnp.zeros((2 * tokens, middle), jnp.float32)
    for tap, patch in enumerate(patches):
        partial = partial + lax.dot_general(
            patch,
            own_half[:, tap * block_in : (tap + 1) * block_in, :],
            (((1, 2), (0, 1)), ((), ())),
            preferred_element_type=jnp.float32,
        )
    partial, temporal_rows = lax.optimization_barrier((partial, temporal_rows))
    temporal_rows = lax.all_gather(temporal_rows, ("xhi", "xlo"), axis=0)
    running = partial[:tokens] + lax.ppermute(partial[tokens:], "core", other_core)
    hidden = jax.nn.gelu(running).astype(jnp.bfloat16)
    group_size = lax.axis_size(FRAME_AXES)
    per_pixel = tokens // group_size
    arrived = lax.all_to_all(
        hidden.reshape(group_size, per_pixel, middle), FRAME_AXES, 0, 0, tiled=True
    )
    group_width = middle // DGROUPS
    frame_sequence = arrived.reshape(FRAMES, per_pixel, DGROUPS, group_width)
    offsets = (jnp.arange(3, dtype=jnp.int32) - 1)[None, :] * dilation[:, None]
    selector_matrix = (
        frame_time[None, None, None, :]
        == frame_time[None, None, :, None] + offsets[:, :, None, None]
    ).astype(jnp.bfloat16)
    stacked_panels = jnp.einsum(
        "gkfe,epgc->fpkgc", selector_matrix, frame_sequence, preferred_element_type=jnp.float32
    )
    stacked_panels = stacked_panels.astype(jnp.bfloat16).reshape(FRAMES * per_pixel, 3, middle)
    xhi, z, xlo, core = channel_dims()
    arrived, temporal_rows = lax.optimization_barrier((arrived, temporal_rows))
    pair = jnp.stack([temporal_rows, lax.ppermute(temporal_rows, "core", other_core)])
    temporal_w = jnp.where(lax.axis_index("core") == 0, pair, pair[::-1])
    temporal_w = temporal_w.reshape(core, xhi, xlo, z, block_out, 3, middle)
    temporal_w = temporal_w.transpose(1, 3, 2, 0, 4, 5, 6).reshape(channels, 3, middle)
    result = lax.dot_general(
        stacked_panels, temporal_w, (((1, 2), (1, 2)), ((), ())), preferred_element_type=jnp.float32
    )
    mixed_out = result.astype(jnp.bfloat16)
    returned = lax.all_to_all(
        mixed_out.reshape(group_size, per_pixel, channels), FRAME_AXES, 0, 0, tiled=True
    )
    update = returned.reshape(rows_dev, cols_dev, channels)
    return (values + update.astype(jnp.float32)).astype(jnp.bfloat16)


def solution(mesh):
    clips = mesh.shape["clip"]
    fine = jax.sharding.Mesh(
        mesh.devices.reshape(clips, 2, -1, 2, 2, 2), ("clip",) + ALL
    )
    return jax.shard_map(
        shards,
        mesh=fine,
        in_specs=(
            P(("clip",) + ST, FS, None),
            P(None, ALL, None),
            P(None, None, ALL),
            P("clip"),
            P("clip"),
        ),
        out_specs=P(("clip",) + ST, FS, None),
        check_vma=False,
    )
```

```python
import jax
import jax.numpy as jnp
from jax import lax
from jax.sharding import PartitionSpec as P

DGROUPS = 8
FRAMES = 16
ROWS = 16
ST = ("xhi", "zhi", "zlo")
FS = ("xlo", "core")
FRAME_AXES = ("xhi", "zhi")
ALL = ("xhi", "zhi", "zlo", "xlo", "core")


def padded_2(cells, sides, width):
    for axis, dim in sides:
        count = lax.axis_size(axis)
        ends = count - 1
        head = lax.slice_in_dim(cells, 0, width, axis=dim)
        tail = lax.slice_in_dim(cells, cells.shape[dim] - width, cells.shape[dim], axis=dim)
        cells = jnp.concatenate(
            [
                lax.ppermute(tail, axis, [(i, (i + 1) % count) for i in range(ends)]),
                cells,
                lax.ppermute(head, axis, [((i + 1) % count, i) for i in range(ends)]),
            ],
            axis=dim,
        )
    return cells


def partner(value, axis, distance):
    mask = 2**distance
    pairs = [(source, source ^ mask) for source in range(lax.axis_size(axis))]
    return lax.ppermute(value, axis, pairs)


def weight_rows(w_spatial, w_temporal):
    middle = w_spatial.shape[2]
    return jnp.concatenate(
        [w_spatial.reshape(-1, middle), w_temporal.transpose(2, 0, 1).reshape(-1, middle)], axis=0
    )


def ring_gather(block, axis):
    count = lax.axis_size(axis)
    up = [(i, (i + 1) % count) for i in range(count)]
    down = [(i, (i - 1) % count) for i in range(count)]
    from_below = lax.ppermute(block, axis, up)
    from_above = lax.ppermute(block, axis, down)
    half = block.shape[1] // 2
    far_low = lax.ppermute(from_below[:, :half], axis, up)
    far_high = lax.ppermute(from_above[:, half:], axis, down)
    far = jnp.concatenate([far_low, far_high], axis=1)
    by_offset = jnp.stack([block, from_above, far, from_below])
    me = lax.axis_index(axis)
    doubled = jnp.concatenate([by_offset, by_offset])
    return lax.dynamic_slice_in_dim(doubled, count - me, count, axis=0)


def channel_dims():
    return (
        lax.axis_size("xhi"),
        lax.axis_size("zhi") * lax.axis_size("zlo"),
        lax.axis_size("xlo"),
        lax.axis_size("core"),
    )


def to_gathered_order(cells, block):
    lead = cells.shape[:-1]
    n = len(lead)
    split = cells.reshape(lead + channel_dims() + (block,))
    order = tuple(range(n)) + (n + 3, n, n + 2, n + 1, n + 4)
    return split.transpose(order).reshape(lead + (-1, block))


def from_gathered_order(cells, block):
    lead = cells.shape[:-1]
    n = len(lead)
    xhi, z, xlo, core = channel_dims()
    split = cells.reshape(lead + (core, xhi, xlo, z, block))
    order = tuple(range(n)) + (n + 1, n + 3, n + 2, n, n + 4)
    return split.transpose(order).reshape(lead + (-1,))


def shards(clip_tokens, w_spatial, w_temporal, frame_time, dilation):
    rows_dev, cols_dev, channels = clip_tokens.shape
    middle = w_spatial.shape[2]
    block_in = w_spatial.shape[1]
    block_out = w_temporal.shape[2]
    spatial_rows = w_spatial.shape[0] * block_in
    along_z = lax.all_gather(weight_rows(w_spatial, w_temporal), ("zhi", "zlo"), axis=0)
    values = clip_tokens.astype(jnp.float32)
    average = jnp.mean(values, axis=-1, keepdims=True)
    kernel_extent = jnp.mean(jnp.square(values - average), axis=-1, keepdims=True)
    normed = ((values - average) * lax.rsqrt(kernel_extent + 1e-06)).astype(jnp.bfloat16)
    normed = to_gathered_order(normed, block_in).reshape(rows_dev, cols_dev, channels)
    widened = padded_2(normed, ((FS, 1),), 1)
    blank_row = jnp.zeros((1,) + widened.shape[1:], jnp.bfloat16)
    lower_half = lax.axis_index(ST) % 2 == 1
    outgoing = jnp.where(lower_half, widened[:1], widened[-1:])
    incoming = partner(outgoing, ST, 0)
    top_rim = jnp.where(lower_half, incoming, blank_row)
    bottom_rim = jnp.where(lower_half, blank_row, incoming)
    padded = jnp.concatenate([top_rim, widened, bottom_rim], axis=0)
    first_row = lax.axis_index(ST) * rows_dev
    in_frame = (first_row + jnp.arange(rows_dev, dtype=jnp.int32)) % ROWS
    masks = []
    for shift_amount in (-1, 0, 1):
        masks.append(
            ((in_frame + shift_amount >= 0) & (in_frame + shift_amount < ROWS)).astype(jnp.bfloat16)
        )
    tokens = rows_dev * cols_dev
    other_core = [(0, 1), (1, 0)]
    partner_padded = lax.ppermute(padded, "core", other_core)
    half_blocks = channels // block_in // lax.axis_size("core")
    start = lax.axis_index("core") * half_blocks
    width = half_blocks * block_in
    own_part = lax.dynamic_slice_in_dim(padded, start * block_in, width, axis=2)
    partner_part = lax.dynamic_slice_in_dim(partner_padded, start * block_in, width, axis=2)
    patches = []
    for row_tap in range(3):
        inside = masks[row_tap][:, None, None]
        mine = own_part[row_tap : row_tap + rows_dev] * inside
        theirs = partner_part[row_tap : row_tap + rows_dev] * inside
        for column_kernel_tap in range(3):
            both = jnp.concatenate(
                [
                    src_tile[:, column_kernel_tap : column_kernel_tap + cols_dev, :]
                    for src_tile in (mine, theirs)
                ]
            )
            patches.append(both.reshape(2 * tokens, -1, block_in))
    early = 3
    along_z, *head = lax.optimization_barrier((along_z, *patches[:early]))
    patches[:early] = head
    cut = 5 * block_in
    parts = [
        lax.all_gather(along_z[:, :cut], ("xhi", "xlo"), axis=0),
        ring_gather(along_z[:, cut:spatial_rows], ("xhi", "xlo")),
    ]
    parts = [part.reshape((-1,) + part.shape[2:]) for part in parts]
    temporal_rows = along_z[:, spatial_rows:]
    partial = jnp.zeros((2 * tokens, middle), jnp.float32)
    for tap, patch in enumerate(patches):
        row = tap * block_in
        partial = partial + lax.dot_general(
            patch,
            parts[row // cut][:, row % cut : row % cut + block_in, :],
            (((1, 2), (0, 1)), ((), ())),
            preferred_element_type=jnp.float32,
        )
    partial, temporal_rows = lax.optimization_barrier((partial, temporal_rows))
    temporal_rows = lax.all_gather(temporal_rows, ("xhi", "xlo"), axis=0)
    running = partial[:tokens] + lax.ppermute(partial[tokens:], "core", other_core)
    hidden = jax.nn.gelu(running).astype(jnp.bfloat16)
    group_size = lax.axis_size(FRAME_AXES)
    per_pixel = tokens // group_size
    arrived = lax.all_to_all(
        hidden.reshape(group_size, per_pixel, middle), FRAME_AXES, 0, 0, tiled=True
    )
    group_width = middle // DGROUPS
    frame_sequence = arrived.reshape(FRAMES, per_pixel, DGROUPS, group_width)
    offsets = (jnp.arange(3, dtype=jnp.int32) - 1)[None, :] * dilation[:, None]
    selector_matrix = (
        frame_time[None, None, None, :]
        == frame_time[None, None, :, None] + offsets[:, :, None, None]
    ).astype(jnp.bfloat16)
    stacked_panels = jnp.einsum(
        "gkfe,epgc->fpkgc", selector_matrix, frame_sequence, preferred_element_type=jnp.float32
    )
    stacked_panels = stacked_panels.astype(jnp.bfloat16).reshape(FRAMES * per_pixel, 3, middle)
    xhi, z, xlo, core = channel_dims()
    arrived, temporal_rows = lax.optimization_barrier((arrived, temporal_rows))
    pair = jnp.stack([temporal_rows, lax.ppermute(temporal_rows, "core", other_core)])
    temporal_w = jnp.where(lax.axis_index("core") == 0, pair, pair[::-1])
    temporal_w = temporal_w.reshape(core, xhi, xlo, z, block_out, 3, middle)
    temporal_w = temporal_w.transpose(1, 3, 2, 0, 4, 5, 6).reshape(channels, 3, middle)
    result = lax.dot_general(
        stacked_panels, temporal_w, (((1, 2), (1, 2)), ((), ())), preferred_element_type=jnp.float32
    )
    mixed_out = result.astype(jnp.bfloat16)
    returned = lax.all_to_all(
        mixed_out.reshape(group_size, per_pixel, channels), FRAME_AXES, 0, 0, tiled=True
    )
    update = returned.reshape(rows_dev, cols_dev, channels)
    return (values + update.astype(jnp.float32)).astype(jnp.bfloat16)


def solution(mesh):
    clips = mesh.shape["clip"]
    fine = jax.sharding.Mesh(
        mesh.devices.reshape(clips, 2, -1, 2, 2, 2), ("clip",) + ALL
    )
    return jax.shard_map(
        shards,
        mesh=fine,
        in_specs=(
            P(("clip",) + ST, FS, None),
            P(None, ALL, None),
            P(None, None, ALL),
            P("clip"),
            P("clip"),
        ),
        out_specs=P(("clip",) + ST, FS, None),
        check_vma=False,
    )
```

```python
import jax
import jax.numpy as jnp
from jax import lax
from jax.sharding import PartitionSpec as P

DGROUPS = 8
FRAMES = 16
ROWS = 16
ST = ("xhi", "zhi", "zlo")
FS = ("xlo", "core")
FRAME_AXES = ("xhi", "zhi")
ALL = ("xhi", "zhi", "zlo", "xlo", "core")


def padded_2(cells, sides, width):
    for axis, dim in sides:
        count = lax.axis_size(axis)
        ends = count - 1
        head = lax.slice_in_dim(cells, 0, width, axis=dim)
        tail = lax.slice_in_dim(cells, cells.shape[dim] - width, cells.shape[dim], axis=dim)
        cells = jnp.concatenate(
            [
                lax.ppermute(tail, axis, [(i, (i + 1) % count) for i in range(ends)]),
                cells,
                lax.ppermute(head, axis, [((i + 1) % count, i) for i in range(ends)]),
            ],
            axis=dim,
        )
    return cells


def partner(value, axis, distance):
    mask = 2**distance
    pairs = [(source, source ^ mask) for source in range(lax.axis_size(axis))]
    return lax.ppermute(value, axis, pairs)


def weight_rows(w_spatial, w_temporal):
    middle = w_spatial.shape[2]
    return jnp.concatenate(
        [w_spatial.reshape(-1, middle), w_temporal.transpose(2, 0, 1).reshape(-1, middle)], axis=0
    )


def channel_dims():
    return (
        lax.axis_size("xhi"),
        lax.axis_size("zhi") * lax.axis_size("zlo"),
        lax.axis_size("xlo"),
        lax.axis_size("core"),
    )


def to_gathered_order(cells, block):
    lead = cells.shape[:-1]
    n = len(lead)
    split = cells.reshape(lead + channel_dims() + (block,))
    order = tuple(range(n)) + (n + 3, n, n + 2, n + 1, n + 4)
    return split.transpose(order).reshape(lead + (-1, block))


def from_gathered_order(cells, block):
    lead = cells.shape[:-1]
    n = len(lead)
    xhi, z, xlo, core = channel_dims()
    split = cells.reshape(lead + (core, xhi, xlo, z, block))
    order = tuple(range(n)) + (n + 1, n + 3, n + 2, n, n + 4)
    return split.transpose(order).reshape(lead + (-1,))


def shards(clip_tokens, w_spatial, w_temporal, frame_time, dilation):
    rows_dev, cols_dev, channels = clip_tokens.shape
    middle = w_spatial.shape[2]
    block_in = w_spatial.shape[1]
    block_out = w_temporal.shape[2]
    spatial_rows = w_spatial.shape[0] * block_in
    along_z = lax.all_gather(weight_rows(w_spatial, w_temporal), ("zhi", "zlo"), axis=0)
    values = clip_tokens.astype(jnp.float32)
    average = jnp.mean(values, axis=-1, keepdims=True)
    kernel_extent = jnp.mean(jnp.square(values - average), axis=-1, keepdims=True)
    normed = ((values - average) * lax.rsqrt(kernel_extent + 1e-06)).astype(jnp.bfloat16)
    normed = to_gathered_order(normed, block_in).reshape(rows_dev, cols_dev, channels)
    widened = padded_2(normed, ((FS, 1),), 1)
    blank_row = jnp.zeros((1,) + widened.shape[1:], jnp.bfloat16)
    lower_half = lax.axis_index(ST) % 2 == 1
    outgoing = jnp.where(lower_half, widened[:1], widened[-1:])
    incoming = partner(outgoing, ST, 0)
    top_rim = jnp.where(lower_half, incoming, blank_row)
    bottom_rim = jnp.where(lower_half, blank_row, incoming)
    padded = jnp.concatenate([top_rim, widened, bottom_rim], axis=0)
    first_row = lax.axis_index(ST) * rows_dev
    in_frame = (first_row + jnp.arange(rows_dev, dtype=jnp.int32)) % ROWS
    masks = []
    for shift_amount in (-1, 0, 1):
        masks.append(
            ((in_frame + shift_amount >= 0) & (in_frame + shift_amount < ROWS)).astype(jnp.bfloat16)
        )
    tokens = rows_dev * cols_dev
    other_core = [(0, 1), (1, 0)]
    partner_padded = lax.ppermute(padded, "core", other_core)
    half_blocks = channels // block_in // lax.axis_size("core")
    start = lax.axis_index("core") * half_blocks
    width = half_blocks * block_in
    own_part = lax.dynamic_slice_in_dim(padded, start * block_in, width, axis=2)
    partner_part = lax.dynamic_slice_in_dim(partner_padded, start * block_in, width, axis=2)
    patches = []
    for row_tap in range(3):
        inside = masks[row_tap][:, None, None]
        mine = own_part[row_tap : row_tap + rows_dev] * inside
        theirs = partner_part[row_tap : row_tap + rows_dev] * inside
        for column_kernel_tap in range(3):
            both = jnp.concatenate(
                [
                    src_tile[:, column_kernel_tap : column_kernel_tap + cols_dev, :]
                    for src_tile in (mine, theirs)
                ]
            )
            patches.append(both.reshape(2 * tokens, width))
    early = 3
    along_z, *head = lax.optimization_barrier((along_z, *patches[:early]))
    patches[:early] = head
    own_half = lax.all_gather(along_z[:, :spatial_rows], ("xhi", "xlo"), axis=0)
    own_half = own_half.reshape((-1, spatial_rows) + along_z.shape[2:])
    temporal_rows = along_z[:, spatial_rows:]
    partial = jnp.zeros((2 * tokens, middle), jnp.float32)
    for tap, patch in enumerate(patches):
        partial = partial + jnp.dot(
            patch,
            own_half[:, tap * block_in : (tap + 1) * block_in, :].reshape(width, middle),
            preferred_element_type=jnp.float32,
        )
    partial, temporal_rows = lax.optimization_barrier((partial, temporal_rows))
    temporal_rows = lax.all_gather(temporal_rows, ("xhi", "xlo"), axis=0)
    running = partial[:tokens] + lax.ppermute(partial[tokens:], "core", other_core)
    hidden = jax.nn.gelu(running).astype(jnp.bfloat16)
    group_size = lax.axis_size(FRAME_AXES)
    per_pixel = tokens // group_size
    arrived = lax.all_to_all(
        hidden.reshape(group_size, per_pixel, middle), FRAME_AXES, 0, 0, tiled=True
    )
    group_width = middle // DGROUPS
    frame_sequence = arrived.reshape(FRAMES, per_pixel, DGROUPS, group_width)
    offsets = (jnp.arange(3, dtype=jnp.int32) - 1)[None, :] * dilation[:, None]
    selector_matrix = (
        frame_time[None, None, None, :]
        == frame_time[None, None, :, None] + offsets[:, :, None, None]
    ).astype(jnp.bfloat16)
    stacked_panels = jnp.einsum(
        "gkfe,epgc->fpkgc", selector_matrix, frame_sequence, preferred_element_type=jnp.float32
    )
    stacked_panels = stacked_panels.astype(jnp.bfloat16).reshape(FRAMES * per_pixel, 3, middle)
    xhi, z, xlo, core = channel_dims()
    arrived, temporal_rows = lax.optimization_barrier((arrived, temporal_rows))
    pair = jnp.stack([temporal_rows, lax.ppermute(temporal_rows, "core", other_core)])
    temporal_w = jnp.where(lax.axis_index("core") == 0, pair, pair[::-1])
    temporal_w = temporal_w.reshape(core, xhi, xlo, z, block_out, 3, middle)
    temporal_w = temporal_w.transpose(1, 3, 2, 0, 4, 5, 6).reshape(channels, 3, middle)
    result = lax.dot_general(
        stacked_panels, temporal_w, (((1, 2), (1, 2)), ((), ())), preferred_element_type=jnp.float32
    )
    mixed_out = result.astype(jnp.bfloat16)
    returned = lax.all_to_all(
        mixed_out.reshape(group_size, per_pixel, channels), FRAME_AXES, 0, 0, tiled=True
    )
    update = returned.reshape(rows_dev, cols_dev, channels)
    return (values + update.astype(jnp.float32)).astype(jnp.bfloat16)


def solution(mesh):
    clips = mesh.shape["clip"]
    fine = jax.sharding.Mesh(
        mesh.devices.reshape(clips, 2, -1, 2, 2, 2), ("clip",) + ALL
    )
    return jax.shard_map(
        shards,
        mesh=fine,
        in_specs=(
            P(("clip",) + ST, FS, None),
            P(None, ALL, None),
            P(None, None, ALL),
            P("clip"),
            P("clip"),
        ),
        out_specs=P(("clip",) + ST, FS, None),
        check_vma=False,
    )
```

```python
import jax
import jax.numpy as jnp
from jax import lax
from jax.sharding import PartitionSpec as P

DGROUPS = 8
FRAMES = 16
ROWS = 16
ST = ("xhi", "zhi", "zlo")
FS = ("xlo", "core")
FRAME_AXES = ("xhi", "zhi")
ALL = ("xhi", "zhi", "zlo", "xlo", "core")


def padded_2(cells, sides, width):
    for axis, dim in sides:
        count = lax.axis_size(axis)
        ends = count - 1
        head = lax.slice_in_dim(cells, 0, width, axis=dim)
        tail = lax.slice_in_dim(cells, cells.shape[dim] - width, cells.shape[dim], axis=dim)
        cells = jnp.concatenate(
            [
                lax.ppermute(tail, axis, [(i, (i + 1) % count) for i in range(ends)]),
                cells,
                lax.ppermute(head, axis, [((i + 1) % count, i) for i in range(ends)]),
            ],
            axis=dim,
        )
    return cells


def partner(value, axis, distance):
    mask = 2**distance
    pairs = [(source, source ^ mask) for source in range(lax.axis_size(axis))]
    return lax.ppermute(value, axis, pairs)


def weight_rows(w_spatial, w_temporal):
    middle = w_spatial.shape[2]
    return jnp.concatenate(
        [w_spatial.reshape(-1, middle), w_temporal.transpose(2, 0, 1).reshape(-1, middle)], axis=0
    )


def channel_dims():
    return (
        lax.axis_size("xhi"),
        lax.axis_size("zhi") * lax.axis_size("zlo"),
        lax.axis_size("xlo"),
        lax.axis_size("core"),
    )


def to_gathered_order(cells, block):
    lead = cells.shape[:-1]
    n = len(lead)
    split = cells.reshape(lead + channel_dims() + (block,))
    order = tuple(range(n)) + (n + 3, n, n + 2, n + 1, n + 4)
    return split.transpose(order).reshape(lead + (-1, block))


def from_gathered_order(cells, block):
    lead = cells.shape[:-1]
    n = len(lead)
    xhi, z, xlo, core = channel_dims()
    split = cells.reshape(lead + (core, xhi, xlo, z, block))
    order = tuple(range(n)) + (n + 1, n + 3, n + 2, n, n + 4)
    return split.transpose(order).reshape(lead + (-1,))


def shards(clip_tokens, w_spatial, w_temporal, frame_time, dilation):
    rows_dev, cols_dev, channels = clip_tokens.shape
    middle = w_spatial.shape[2]
    block_in = w_spatial.shape[1]
    block_out = w_temporal.shape[2]
    spatial_rows = w_spatial.shape[0] * block_in
    along_z = lax.all_gather(weight_rows(w_spatial, w_temporal), ("zhi", "zlo"), axis=0)
    values = clip_tokens.astype(jnp.float32)
    average = jnp.mean(values, axis=-1, keepdims=True)
    kernel_extent = jnp.mean(jnp.square(values - average), axis=-1, keepdims=True)
    normed = ((values - average) * lax.rsqrt(kernel_extent + 1e-06)).astype(jnp.bfloat16)
    normed = to_gathered_order(normed, block_in).reshape(rows_dev, cols_dev, channels)
    widened = padded_2(normed, ((FS, 1),), 1)
    blank_row = jnp.zeros((1,) + widened.shape[1:], jnp.bfloat16)
    lower_half = lax.axis_index(ST) % 2 == 1
    outgoing = jnp.where(lower_half, widened[:1], widened[-1:])
    incoming = partner(outgoing, ST, 0)
    top_rim = jnp.where(lower_half, incoming, blank_row)
    bottom_rim = jnp.where(lower_half, blank_row, incoming)
    padded = jnp.concatenate([top_rim, widened, bottom_rim], axis=0)
    first_row = lax.axis_index(ST) * rows_dev
    in_frame = (first_row + jnp.arange(rows_dev, dtype=jnp.int32)) % ROWS
    masks = []
    for shift_amount in (-1, 0, 1):
        masks.append(
            ((in_frame + shift_amount >= 0) & (in_frame + shift_amount < ROWS)).astype(jnp.bfloat16)
        )
    tokens = rows_dev * cols_dev
    other_core = [(0, 1), (1, 0)]
    partner_padded = lax.ppermute(padded, "core", other_core)
    half_blocks = channels // block_in // lax.axis_size("core")
    start = lax.axis_index("core") * half_blocks
    width = half_blocks * block_in
    own_part = lax.dynamic_slice_in_dim(padded, start * block_in, width, axis=2)
    partner_part = lax.dynamic_slice_in_dim(partner_padded, start * block_in, width, axis=2)
    patches = []
    for row_tap in range(3):
        inside = masks[row_tap][:, None, None]
        mine = own_part[row_tap : row_tap + rows_dev] * inside
        theirs = partner_part[row_tap : row_tap + rows_dev] * inside
        for column_kernel_tap in range(3):
            both = jnp.concatenate(
                [
                    src_tile[:, column_kernel_tap : column_kernel_tap + cols_dev, :]
                    for src_tile in (mine, theirs)
                ]
            )
            patches.append(both.reshape(2 * tokens, width))
    early = 3
    along_z, *head = lax.optimization_barrier((along_z, *patches[:early]))
    patches[:early] = head
    own_half = lax.all_gather(along_z[:, :spatial_rows], ("xhi", "xlo"), axis=0)
    own_half = own_half.reshape((-1, spatial_rows) + along_z.shape[2:])
    temporal_rows = along_z[:, spatial_rows:]
    partial = jnp.zeros((2 * tokens, middle), jnp.float32)
    for tap, patch in enumerate(patches):
        partial = partial + jnp.dot(
            patch,
            own_half[:, tap * block_in : (tap + 1) * block_in, :].reshape(width, middle),
            preferred_element_type=jnp.float32,
        )
    partial, temporal_rows = lax.optimization_barrier((partial, temporal_rows))
    temporal_rows = lax.all_gather(temporal_rows, ("xhi", "xlo"), axis=0)
    running = partial[:tokens] + lax.ppermute(partial[tokens:], "core", other_core)
    hidden = jax.nn.gelu(running).astype(jnp.bfloat16)
    group_size = lax.axis_size(FRAME_AXES)
    per_pixel = tokens // group_size
    arrived = lax.all_to_all(
        hidden.reshape(group_size, per_pixel, middle), FRAME_AXES, 0, 0, tiled=True
    )
    group_width = middle // DGROUPS
    frame_sequence = arrived.reshape(FRAMES, per_pixel, DGROUPS, group_width)
    offsets = (jnp.arange(3, dtype=jnp.int32) - 1)[None, :] * dilation[:, None]
    selector_matrix = (
        frame_time[None, None, None, :]
        == frame_time[None, None, :, None] + offsets[:, :, None, None]
    ).astype(jnp.bfloat16)
    stacked_panels = jnp.einsum(
        "gkfe,epgc->fpkgc", selector_matrix, frame_sequence, preferred_element_type=jnp.float32
    )
    stacked_panels = stacked_panels.astype(jnp.bfloat16).reshape(FRAMES * per_pixel, 3, middle)
    xhi, z, xlo, core = channel_dims()
    stacked_panels, temporal_rows = lax.optimization_barrier((stacked_panels, temporal_rows))
    pair = jnp.stack([temporal_rows, lax.ppermute(temporal_rows, "core", other_core)])
    temporal_w = jnp.where(lax.axis_index("core") == 0, pair, pair[::-1])
    temporal_w = temporal_w.reshape(core, xhi, xlo, z, block_out, 3, middle)
    temporal_w = temporal_w.transpose(1, 3, 2, 0, 4, 5, 6).reshape(channels, 3, middle)
    result = lax.dot_general(
        stacked_panels, temporal_w, (((1, 2), (1, 2)), ((), ())), preferred_element_type=jnp.float32
    )
    mixed_out = result.astype(jnp.bfloat16)
    returned = lax.all_to_all(
        mixed_out.reshape(group_size, per_pixel, channels), FRAME_AXES, 0, 0, tiled=True
    )
    update = returned.reshape(rows_dev, cols_dev, channels)
    return (values + update.astype(jnp.float32)).astype(jnp.bfloat16)


def solution(mesh):
    clips = mesh.shape["clip"]
    fine = jax.sharding.Mesh(
        mesh.devices.reshape(clips, 2, -1, 2, 2, 2), ("clip",) + ALL
    )
    return jax.shard_map(
        shards,
        mesh=fine,
        in_specs=(
            P(("clip",) + ST, FS, None),
            P(None, ALL, None),
            P(None, None, ALL),
            P("clip"),
            P("clip"),
        ),
        out_specs=P(("clip",) + ST, FS, None),
        check_vma=False,
    )
```

```python
import jax
import jax.numpy as jnp
from jax import lax
from jax.sharding import PartitionSpec as P

DGROUPS = 8
FRAMES = 16
ROWS = 16
ST = ("xhi", "zhi", "zlo")
FS = ("xlo", "core")
FRAME_AXES = ("xhi", "zhi")
ALL = ("xhi", "zhi", "zlo", "xlo", "core")


def padded_2(cells, sides, width):
    for axis, dim in sides:
        count = lax.axis_size(axis)
        ends = count - 1
        head = lax.slice_in_dim(cells, 0, width, axis=dim)
        tail = lax.slice_in_dim(cells, cells.shape[dim] - width, cells.shape[dim], axis=dim)
        cells = jnp.concatenate(
            [
                lax.ppermute(tail, axis, [(i, (i + 1) % count) for i in range(ends)]),
                cells,
                lax.ppermute(head, axis, [((i + 1) % count, i) for i in range(ends)]),
            ],
            axis=dim,
        )
    return cells


def partner(value, axis, distance):
    mask = 2**distance
    pairs = [(source, source ^ mask) for source in range(lax.axis_size(axis))]
    return lax.ppermute(value, axis, pairs)


def weight_rows(w_spatial, w_temporal):
    middle = w_spatial.shape[2]
    return jnp.concatenate(
        [w_spatial.reshape(-1, middle), w_temporal.transpose(2, 0, 1).reshape(-1, middle)], axis=0
    )


def channel_dims():
    return (
        lax.axis_size("xhi"),
        lax.axis_size("zhi") * lax.axis_size("zlo"),
        lax.axis_size("xlo"),
        lax.axis_size("core"),
    )


def to_gathered_order(cells, block):
    lead = cells.shape[:-1]
    n = len(lead)
    split = cells.reshape(lead + channel_dims() + (block,))
    order = tuple(range(n)) + (n + 3, n, n + 2, n + 1, n + 4)
    return split.transpose(order).reshape(lead + (-1, block))


def from_gathered_order(cells, block):
    lead = cells.shape[:-1]
    n = len(lead)
    xhi, z, xlo, core = channel_dims()
    split = cells.reshape(lead + (core, xhi, xlo, z, block))
    order = tuple(range(n)) + (n + 1, n + 3, n + 2, n, n + 4)
    return split.transpose(order).reshape(lead + (-1,))


def shards(clip_tokens, w_spatial, w_temporal, frame_time, dilation):
    rows_dev, cols_dev, channels = clip_tokens.shape
    middle = w_spatial.shape[2]
    block_in = w_spatial.shape[1]
    block_out = w_temporal.shape[2]
    spatial_rows = w_spatial.shape[0] * block_in
    along_z = lax.all_gather(weight_rows(w_spatial, w_temporal), ("zhi", "zlo"), axis=0)
    values = clip_tokens.astype(jnp.float32)
    average = jnp.mean(values, axis=-1, keepdims=True)
    kernel_extent = jnp.mean(jnp.square(values - average), axis=-1, keepdims=True)
    normed = ((values - average) * lax.rsqrt(kernel_extent + 1e-06)).astype(jnp.bfloat16)
    normed = to_gathered_order(normed, block_in).reshape(rows_dev, cols_dev, channels)
    widened = padded_2(normed, ((FS, 1),), 1)
    blank_row = jnp.zeros((1,) + widened.shape[1:], jnp.bfloat16)
    lower_half = lax.axis_index(ST) % 2 == 1
    outgoing = jnp.where(lower_half, widened[:1], widened[-1:])
    incoming = partner(outgoing, ST, 0)
    top_rim = jnp.where(lower_half, incoming, blank_row)
    bottom_rim = jnp.where(lower_half, blank_row, incoming)
    padded = jnp.concatenate([top_rim, widened, bottom_rim], axis=0)
    first_row = lax.axis_index(ST) * rows_dev
    in_frame = (first_row + jnp.arange(rows_dev, dtype=jnp.int32)) % ROWS
    masks = []
    for shift_amount in (-1, 0, 1):
        masks.append(
            ((in_frame + shift_amount >= 0) & (in_frame + shift_amount < ROWS)).astype(jnp.bfloat16)
        )
    tokens = rows_dev * cols_dev
    other_core = [(0, 1), (1, 0)]
    partner_padded = lax.ppermute(padded, "core", other_core)
    half_blocks = channels // block_in // lax.axis_size("core")
    start = lax.axis_index("core") * half_blocks
    width = half_blocks * block_in
    own_part = lax.dynamic_slice_in_dim(padded, start * block_in, width, axis=2)
    partner_part = lax.dynamic_slice_in_dim(partner_padded, start * block_in, width, axis=2)
    patches = []
    for row_tap in range(3):
        inside = masks[row_tap][:, None, None]
        mine = own_part[row_tap : row_tap + rows_dev] * inside
        theirs = partner_part[row_tap : row_tap + rows_dev] * inside
        for column_kernel_tap in range(3):
            both = jnp.concatenate(
                [
                    src_tile[:, column_kernel_tap : column_kernel_tap + cols_dev, :]
                    for src_tile in (mine, theirs)
                ]
            )
            patches.append(both.reshape(2 * tokens, width))
    early = 3
    along_z, *head = lax.optimization_barrier((along_z, *patches[:early]))
    patches[:early] = head
    cut = 5 * block_in
    parts = [
        lax.all_gather(along_z[:, rows], ("xhi", "xlo"), axis=0)
        for rows in (slice(None, cut), slice(cut, spatial_rows))
    ]
    parts = [part.reshape((-1,) + part.shape[2:]) for part in parts]
    temporal_rows = along_z[:, spatial_rows:]
    partial = jnp.zeros((2 * tokens, middle), jnp.float32)
    for tap, patch in enumerate(patches):
        row = tap * block_in
        partial = partial + jnp.dot(
            patch,
            parts[row // cut][:, row % cut : row % cut + block_in, :].reshape(width, middle),
            preferred_element_type=jnp.float32,
        )
    partial, temporal_rows = lax.optimization_barrier((partial, temporal_rows))
    temporal_rows = lax.all_gather(temporal_rows, ("xhi", "xlo"), axis=0)
    running = partial[:tokens] + lax.ppermute(partial[tokens:], "core", other_core)
    hidden = jax.nn.gelu(running).astype(jnp.bfloat16)
    group_size = lax.axis_size(FRAME_AXES)
    per_pixel = tokens // group_size
    arrived = lax.all_to_all(
        hidden.reshape(group_size, per_pixel, middle), FRAME_AXES, 0, 0, tiled=True
    )
    group_width = middle // DGROUPS
    frame_sequence = arrived.reshape(FRAMES, per_pixel, DGROUPS, group_width)
    offsets = (jnp.arange(3, dtype=jnp.int32) - 1)[None, :] * dilation[:, None]
    selector_matrix = (
        frame_time[None, None, None, :]
        == frame_time[None, None, :, None] + offsets[:, :, None, None]
    ).astype(jnp.bfloat16)
    stacked_panels = jnp.einsum(
        "gkfe,epgc->fpkgc", selector_matrix, frame_sequence, preferred_element_type=jnp.float32
    )
    stacked_panels = stacked_panels.astype(jnp.bfloat16).reshape(FRAMES * per_pixel, 3, middle)
    xhi, z, xlo, core = channel_dims()
    stacked_panels, temporal_rows = lax.optimization_barrier((stacked_panels, temporal_rows))
    pair = jnp.stack([temporal_rows, lax.ppermute(temporal_rows, "core", other_core)])
    temporal_w = jnp.where(lax.axis_index("core") == 0, pair, pair[::-1])
    temporal_w = temporal_w.reshape(core, xhi, xlo, z, block_out, 3, middle)
    temporal_w = temporal_w.transpose(1, 3, 2, 0, 4, 5, 6).reshape(channels, 3, middle)
    result = lax.dot_general(
        stacked_panels, temporal_w, (((1, 2), (1, 2)), ((), ())), preferred_element_type=jnp.float32
    )
    mixed_out = result.astype(jnp.bfloat16)
    returned = lax.all_to_all(
        mixed_out.reshape(group_size, per_pixel, channels), FRAME_AXES, 0, 0, tiled=True
    )
    update = returned.reshape(rows_dev, cols_dev, channels)
    return (values + update.astype(jnp.float32)).astype(jnp.bfloat16)


def solution(mesh):
    clips = mesh.shape["clip"]
    fine = jax.sharding.Mesh(
        mesh.devices.reshape(clips, 2, -1, 2, 2, 2), ("clip",) + ALL
    )
    return jax.shard_map(
        shards,
        mesh=fine,
        in_specs=(
            P(("clip",) + ST, FS, None),
            P(None, ALL, None),
            P(None, None, ALL),
            P("clip"),
            P("clip"),
        ),
        out_specs=P(("clip",) + ST, FS, None),
        check_vma=False,
    )
```
